256 devices in a mesh: tm: 32 (over y, x, core), inner: 8 (over z).
Axes of the slice: x: 4, y: 4, z: 8, core: 2. Of those that a mesh axis runs over, the one named last changes fastest.
Arguments:
- query_input: bfloat16 [32768, 1792], P(('tm', 'inner')), may hold values from -6 to 6
- key_input: bfloat16 [32768, 1792], P(('tm', 'inner')), may hold values from -6 to 6
- value_input: bfloat16 [32768, 1792], P(('tm', 'inner')), may hold values from -6 to 6
- cotangent: bfloat16 [32768, 1792], P(('tm', 'inner')), may hold values from -6 to 6
- span_labels: int32 [32768], P(('tm', 'inner')), may hold values from 0 to 6, as said below
Outputs:
- query_gradient: bfloat16 [32768, 1792], P(('tm', 'inner'))
- key_gradient: bfloat16 [32768, 1792], P(('tm', 'inner'))
- value_gradient: bfloat16 [32768, 1792], P(('tm', 'inner'))
The draws below stay inside these ranges and needn't reach their ends.
Inputs may be any that keep to these rules, and one draw needn't show every extreme that they name: `span_labels`: span labels never fall along the tokens; each of the 7 spans holds 1 to 8 whole frames of 1024 tokens and begins at a multiple of 1024; one span holds exactly 8192 tokens.
All inputs are finite; a program needn't handle non-finite values.
Results may differ from the reference program's by a relative error of at most 0.008.
Values may be sent and summed in bfloat16 or wider, within the bound.
No kernel may reach another device: no remote copies, remote signals or barrier semaphores. Data moves between devices by JAX's collectives and lax.ppermute only.
A program may use at most 192 MiB of HBM per device.

```python
import jax
import jax.numpy as jnp
from jax import lax

HEADS = 16
DH = 112
SPANS = 7
TOKENS = 32768
FRAME = 1024


def draw_span_labels(key, part):
    first_key, second_key = jax.random.split(key)
    largest_slot = jax.random.randint(first_key, (), 0, SPANS)
    others = jnp.full((SPANS - 1,), 4, jnp.int32)
    move_keys = jax.random.split(second_key, 12)
    for step in range(12):
        picked = jax.random.randint(move_keys[step], (2,), 0, SPANS - 1)
        source = picked[0]
        target = picked[1]
        allowed = (source != target) & (others[source] > 1) & (others[target] < 8)
        amount = allowed.astype(jnp.int32)
        others = others.at[source].add(-amount)
        others = others.at[target].add(amount)
    positions = jnp.arange(SPANS, dtype=jnp.int32)
    shifted = jnp.clip(jnp.where(positions < largest_slot, positions, positions - 1), 0, SPANS - 2)
    lengths = jnp.where(positions == largest_slot, 8, others[shifted])
    bounds = jnp.cumsum(lengths)
    frames = jnp.arange(32, dtype=jnp.int32)
    frame_label = jnp.sum((frames[:, None] >= bounds[None, :-1]).astype(jnp.int32), axis=1)
    return jnp.repeat(frame_label, FRAME, total_repeat_length=32 * FRAME).astype(jnp.int32)


def block_scale(rng, dims, cuts, least, high):
    def one(position, parts):
        heights = jax.random.uniform(jax.random.fold_in(jax.random.fold_in(rng, 6), position), (parts,), jnp.float32, least / len(cuts), high / len(cuts))
        return jnp.repeat(jnp.exp(heights), dims[position] // parts).reshape((-1,) + (1,) * (len(dims) - position - 1))

    gain = one(*cuts[0])
    for cut in cuts[1:]:
        gain = gain * one(*cut)
    return gain


def normal_values(key, extent, width, most, cuts=(), kind=jnp.bfloat16):
    drawn = jax.random.normal(key, extent, jnp.float32) * width
    if len(cuts) > 0:
        drawn = block_scale(key, extent, cuts, -0.22, 0.18) * drawn
    return jnp.clip(drawn, min=-most, max=most).astype(kind)


def setup_inputs(seed: int = 0) -> dict:
    streams_of = jax.random.split(jax.random.key(seed), 6)
    query_input = normal_values(streams_of[0], (TOKENS, HEADS * DH), 1.0, 6.0, ((0, 256),))
    key_input = normal_values(streams_of[1], (TOKENS, HEADS * DH), 1.0, 6.0, ((0, 256),))
    value_input = normal_values(streams_of[2], (TOKENS, HEADS * DH), 1.0, 6.0, ((0, 256),))
    cotangent = normal_values(streams_of[3], (TOKENS, HEADS * DH), 1.0, 6.0, ((0, 256),))
    span_labels = draw_span_labels(jax.random.fold_in(streams_of[5], 71), 0)
    return dict(query_input=query_input, key_input=key_input, value_input=value_input, cotangent=cotangent, span_labels=span_labels)


loss_scale = 1024.0
exact = lax.Precision.HIGHEST


def round_low(values_in):
    return lax.optimization_barrier(values_in.astype(jnp.bfloat16)).astype(jnp.float32)


def reverse_cumsum(pieces):
    return jnp.flip(jnp.cumsum(jnp.flip(pieces, 0), 0), 0)


def reference(query_input, key_input, value_input, cotangent, span_labels):
    token_count = query_input.shape[0]
    levels = jnp.arange(SPANS, dtype=jnp.int32)
    onehot = (span_labels[:, None] == levels[None, :]).astype(jnp.float32)

    def split_heads(flat):
        return jnp.transpose(flat.reshape(token_count, HEADS, DH), (1, 0, 2))

    def per_head(pieces):
        query_head, key_head, value_head, cot_head = pieces
        feat_query = jnp.maximum(query_head, 0).astype(jnp.float32)
        feat_key = jnp.maximum(key_head, 0).astype(jnp.float32)
        value_full = value_head.astype(jnp.float32)
        key_spread = onehot[:, :, None] * feat_key[:, None, :]
        state_part = jnp.einsum("tck,tv->ckv", key_spread, value_full, precision=exact)
        mass_part = jnp.einsum("tc,tk->ck", onehot, feat_key, precision=exact)
        state_low = round_low(jnp.cumsum(state_part, 0))
        mass_low = round_low(jnp.cumsum(mass_part, 0))
        query_spread = onehot[:, :, None] * feat_query[:, None, :]
        numerator = jnp.einsum("tck,ckv->tv", query_spread, state_low, precision=exact)
        weight = jnp.einsum("tck,ck->t", query_spread, mass_low, precision=exact)
        denominator = weight / DH + 1.0
        output = numerator / (DH * denominator[:, None])
        scaled = cot_head.astype(jnp.float32) * loss_scale
        numer_back = round_low(scaled / (DH * denominator[:, None]))
        weight_back = round_low(-jnp.sum(scaled * output, axis=-1) / (DH * denominator))
        adjoint_part = jnp.einsum("tck,tv->ckv", query_spread, numer_back, precision=exact)
        adjoint_mass = jnp.einsum("tck,t->ck", query_spread, weight_back, precision=exact)
        adjoint_low = round_low(reverse_cumsum(adjoint_part))
        adjoint_mass_low = round_low(reverse_cumsum(adjoint_mass))
        back_spread = onehot[:, :, None] * numer_back[:, None, :]
        query_feat = jnp.einsum("tcv,ckv->tk", back_spread, state_low, precision=exact)
        query_feat = query_feat + jnp.dot(onehot, mass_low, precision=exact) * weight_back[:, None]
        value_spread = onehot[:, :, None] * value_full[:, None, :]
        key_feat = jnp.einsum("tcv,ckv->tk", value_spread, adjoint_low, precision=exact)
        key_feat = key_feat + jnp.dot(onehot, adjoint_mass_low, precision=exact)
        value_back = jnp.einsum("tck,ckv->tv", key_spread, adjoint_low, precision=exact)
        query_back = jnp.where(query_head > 0, query_feat, 0.0).astype(jnp.bfloat16)
        key_back = jnp.where(key_head > 0, key_feat, 0.0).astype(jnp.bfloat16)
        return query_back, key_back, value_back.astype(jnp.bfloat16)

    results = lax.map(per_head, (split_heads(query_input), split_heads(key_input), split_heads(value_input), split_heads(cotangent)))

    def merge_heads(stacked):
        return jnp.transpose(stacked, (1, 0, 2)).reshape(token_count, HEADS * DH)

    return merge_heads(results[0]), merge_heads(results[1]), merge_heads(results[2])
```

```python
import jax
import jax.numpy as jnp
from jax import lax
from jax.sharding import PartitionSpec as P

DH = 112
SPANS = 7

loss_scale = 1024.0


def visible(part, label, later):
    own = lax.psum_scatter(part, "inner", scatter_dimension=0, tiled=True)
    levels = jnp.arange(SPANS, dtype=jnp.int32)
    onehot = (levels == label).astype(jnp.float32)
    spread = onehot[:, None, None, None] * own[None]
    totals = lax.psum(spread, "tm")
    keep = (levels >= label) if later else (levels <= label)
    seen = jnp.sum(jnp.where(keep[:, None, None, None], totals, 0.0), axis=0)
    return lax.all_gather(seen.astype(jnp.bfloat16), "inner", axis=0, tiled=True)


def local(query_input, key_input, value_input, cotangent, span_labels):
    tokens = query_input.shape[0]
    heads = query_input.shape[1] // DH

    def split(flat):
        return flat.reshape(tokens, heads, DH)

    query_heads = split(query_input)
    key_heads = split(key_input)
    value_heads = split(value_input)
    feat_query = jnp.maximum(query_heads, 0)
    feat_key = jnp.maximum(key_heads, 0)
    label = span_labels[0]
    ones = jnp.ones((tokens, heads, 1), jnp.bfloat16)
    value_aug = jnp.concatenate([value_heads, ones], axis=-1)
    state_part = jnp.einsum(
        "thk,thv->hkv", feat_key, value_aug, preferred_element_type=jnp.float32
    )
    state_vis = visible(state_part, label, False)
    both = jnp.einsum("thk,hkv->thv", feat_query, state_vis, preferred_element_type=jnp.float32)
    numerator = both[..., :DH]
    weight = both[..., DH]
    denominator = weight / DH + 1.0
    output = numerator / (DH * denominator[..., None])
    scaled = split(cotangent).astype(jnp.float32) * loss_scale
    numer_back = (scaled / (DH * denominator[..., None])).astype(jnp.bfloat16)
    weight_back = (-jnp.sum(scaled * output, axis=-1) / (DH * denominator)).astype(jnp.bfloat16)
    back_aug = jnp.concatenate([numer_back, weight_back[..., None]], axis=-1)
    adjoint_part = jnp.einsum(
        "thk,thv->hkv", feat_query, back_aug, preferred_element_type=jnp.float32
    )
    adjoint_vis = visible(adjoint_part, label, True)
    query_feat = jnp.einsum("thv,hkv->thk", back_aug, state_vis, preferred_element_type=jnp.float32)
    key_feat = jnp.einsum("thv,hkv->thk", value_aug, adjoint_vis, preferred_element_type=jnp.float32)
    value_back = jnp.einsum(
        "thk,hkv->thv", feat_key, adjoint_vis[..., :DH], preferred_element_type=jnp.float32
    )
    query_back = jnp.where(query_heads > 0, query_feat, 0.0).astype(jnp.bfloat16)
    key_back = jnp.where(key_heads > 0, key_feat, 0.0).astype(jnp.bfloat16)

    def merge(heads_arr):
        return heads_arr.reshape(tokens, heads * DH)

    return merge(query_back), merge(key_back), merge(value_back.astype(jnp.bfloat16))


def solution(mesh):
    row = P(("tm", "inner"), None)
    return jax.shard_map(
        local,
        mesh=mesh,
        in_specs=(row, row, row, row, P(("tm", "inner"))),
        out_specs=(row, row, row),
        check_vma=False,
    )
```

```python
import jax
import jax.numpy as jnp
from jax import lax
from jax.sharding import PartitionSpec as P

DH = 112

loss_scale = 1024.0


def visible(part, label, later):
    tag = jnp.broadcast_to(label.astype(jnp.float32), part.shape[:-1] + (1,))
    packed = jnp.concatenate([part, tag], axis=-1)
    every = lax.all_gather(packed, "tm", axis=0)
    their = every[:, 0, 0, DH + 1]
    keep = (their >= label) if later else (their <= label)
    seen = jnp.sum(jnp.where(keep[:, None, None, None], every[..., : DH + 1], 0.0), axis=0)
    return seen.astype(jnp.bfloat16)


def local(query_input, key_input, value_input, cotangent, span_labels):
    groups = lax.axis_size("inner")
    rows, columns = query_input.shape
    width = columns // groups
    heads = width // DH
    tokens = rows * groups

    stacked = jnp.stack([query_input, key_input, value_input, cotangent])
    outgoing = stacked.reshape(4, rows, groups, width).transpose(2, 0, 1, 3)
    incoming = lax.all_to_all(outgoing, "inner", 0, 0, tiled=True)
    arrived = incoming.transpose(1, 0, 2, 3).reshape(4, tokens, heads, DH)
    query_heads, key_heads, value_heads, cotangent_heads = (
        arrived[0],
        arrived[1],
        arrived[2],
        arrived[3],
    )

    feat_query = jnp.maximum(query_heads, 0)
    feat_key = jnp.maximum(key_heads, 0)
    label = span_labels[0]
    ones = jnp.ones((tokens, heads, 1), jnp.bfloat16)
    value_aug = jnp.concatenate([value_heads, ones], axis=-1)
    state_part = jnp.einsum(
        "thk,thv->hkv", feat_key, value_aug, preferred_element_type=jnp.float32
    )
    state_vis = visible(state_part, label, False)
    both = jnp.einsum("thk,hkv->thv", feat_query, state_vis, preferred_element_type=jnp.float32)
    numerator = both[..., :DH]
    weight = both[..., DH]
    denominator = weight / DH + 1.0
    output = numerator / (DH * denominator[..., None])
    scaled = cotangent_heads.astype(jnp.float32) * loss_scale
    numer_back = (scaled / (DH * denominator[..., None])).astype(jnp.bfloat16)
    weight_back = (-jnp.sum(scaled * output, axis=-1) / (DH * denominator)).astype(jnp.bfloat16)
    back_aug = jnp.concatenate([numer_back, weight_back[..., None]], axis=-1)
    adjoint_part = jnp.einsum(
        "thk,thv->hkv", feat_query, back_aug, preferred_element_type=jnp.float32
    )
    adjoint_vis = visible(adjoint_part, label, True)
    query_feat = jnp.einsum("thv,hkv->thk", back_aug, state_vis, preferred_element_type=jnp.float32)
    key_feat = jnp.einsum("thv,hkv->thk", value_aug, adjoint_vis, preferred_element_type=jnp.float32)
    value_back = jnp.einsum(
        "thk,hkv->thv", feat_key, adjoint_vis[..., :DH], preferred_element_type=jnp.float32
    )
    query_back = jnp.where(query_heads > 0, query_feat, 0.0).astype(jnp.bfloat16)
    key_back = jnp.where(key_heads > 0, key_feat, 0.0).astype(jnp.bfloat16)

    results = jnp.stack([query_back, key_back, value_back.astype(jnp.bfloat16)])
    leaving = results.reshape(3, groups, rows, width).transpose(1, 0, 2, 3)
    returned = lax.all_to_all(leaving, "inner", 0, 0, tiled=True)
    merged = returned.transpose(1, 2, 0, 3).reshape(3, rows, columns)
    return merged[0], merged[1], merged[2]


def solution(mesh):
    row = P(("tm", "inner"), None)
    return jax.shard_map(
        local,
        mesh=mesh,
        in_specs=(row, row, row, row, P(("tm", "inner"))),
        out_specs=(row, row, row),
        check_vma=False,
    )
```

```python
import functools

import jax
import jax.numpy as jnp
from jax import lax
from jax.sharding import PartitionSpec as P

DH = 112

loss_scale = 1024.0


ROW = 8


def shifted(value, count, step):
    total = lax.axis_size("tm")
    pairs = []
    for base in range(0, total, count):
        for i in range(count):
            pairs.append((base + i, base + (i + step) % count))
    return lax.ppermute(value, "tm", pairs)


def strided(value, stride, step):
    total = lax.axis_size("tm")
    rows = total // stride
    pairs = []
    for r in range(rows):
        for j in range(stride):
            pairs.append((r * stride + j, ((r + step) % rows) * stride + j))
    return lax.ppermute(value, "tm", pairs)


def visible(part, label, later):
    total = lax.axis_size("tm")
    row = min(ROW, total)
    rows = total // row
    me = lax.axis_index("tm") // row
    flabel = label.astype(jnp.float32)
    tag = jnp.broadcast_to(flabel, part.shape[:-1] + (1,))
    packed = jnp.concatenate([part, tag], axis=-1)
    frames = [packed] + [shifted(packed, row, s) for s in range(1, row)]
    labels = [f[0, 0, DH + 1] for f in frames]
    states = [f[..., : DH + 1] for f in frames]
    keep = [(l >= flabel) if later else (l <= flabel) for l in labels]
    seen = sum(jnp.where(k, s, 0.0) for k, s in zip(keep, states))
    if rows > 1:
        edge = functools.reduce(jnp.maximum, labels) if later else functools.reduce(jnp.minimum, labels)
        whole = sum(states)
        edge_sum = sum(jnp.where(l == edge, s, 0.0) for l, s in zip(labels, states))
        etag = jnp.broadcast_to(edge, part.shape[:-1] + (1,))
        summary = jnp.stack(
            [jnp.concatenate([whole, etag], -1), jnp.concatenate([edge_sum, etag], -1)]
        )
        for s in range(1, rows):
            got = strided(summary, row, s)
            source = (me - s) % rows
            their_edge = got[1, 0, 0, DH + 1]
            full = (source > me) if later else (source < me)
            part_only = ((source < me) if later else (source > me)) & (their_edge == flabel)
            seen = (
                seen
                + jnp.where(full, got[0, ..., : DH + 1], 0.0)
                + jnp.where(part_only, got[1, ..., : DH + 1], 0.0)
            )
    return seen.astype(jnp.bfloat16)


def local(query_input, key_input, value_input, cotangent, span_labels):
    groups = lax.axis_size("inner")
    rows, columns = query_input.shape
    width = columns // groups
    heads = width // DH
    tokens = rows * groups

    stacked = jnp.stack([query_input, key_input, value_input, cotangent])
    outgoing = stacked.reshape(4, rows, groups, width).transpose(2, 0, 1, 3)
    incoming = lax.all_to_all(outgoing, "inner", 0, 0, tiled=True)
    arrived = incoming.transpose(1, 0, 2, 3).reshape(4, tokens, heads, DH)
    query_heads, key_heads, value_heads, cotangent_heads = (
        arrived[0],
        arrived[1],
        arrived[2],
        arrived[3],
    )

    feat_query = jnp.maximum(query_heads, 0)
    feat_key = jnp.maximum(key_heads, 0)
    label = span_labels[0]
    ones = jnp.ones((tokens, heads, 1), jnp.bfloat16)
    value_aug = jnp.concatenate([value_heads, ones], axis=-1)
    state_part = jnp.einsum(
        "thk,thv->hkv", feat_key, value_aug, preferred_element_type=jnp.float32
    )
    state_vis = visible(state_part, label, False)
    both = jnp.einsum("thk,hkv->thv", feat_query, state_vis, preferred_element_type=jnp.float32)
    numerator = both[..., :DH]
    weight = both[..., DH]
    denominator = weight / DH + 1.0
    output = numerator / (DH * denominator[..., None])
    scaled = cotangent_heads.astype(jnp.float32) * loss_scale
    numer_back = (scaled / (DH * denominator[..., None])).astype(jnp.bfloat16)
    weight_back = (-jnp.sum(scaled * output, axis=-1) / (DH * denominator)).astype(jnp.bfloat16)
    back_aug = jnp.concatenate([numer_back, weight_back[..., None]], axis=-1)
    adjoint_part = jnp.einsum(
        "thk,thv->hkv", feat_query, back_aug, preferred_element_type=jnp.float32
    )
    adjoint_vis = visible(adjoint_part, label, True)
    query_feat = jnp.einsum("thv,hkv->thk", back_aug, state_vis, preferred_element_type=jnp.float32)
    key_feat = jnp.einsum("thv,hkv->thk", value_aug, adjoint_vis, preferred_element_type=jnp.float32)
    value_back = jnp.einsum(
        "thk,hkv->thv", feat_key, adjoint_vis[..., :DH], preferred_element_type=jnp.float32
    )
    query_back = jnp.where(query_heads > 0, query_feat, 0.0).astype(jnp.bfloat16)
    key_back = jnp.where(key_heads > 0, key_feat, 0.0).astype(jnp.bfloat16)

    results = jnp.stack([query_back, key_back, value_back.astype(jnp.bfloat16)])
    leaving = results.reshape(3, groups, rows, width).transpose(1, 0, 2, 3)
    returned = lax.all_to_all(leaving, "inner", 0, 0, tiled=True)
    merged = returned.transpose(1, 2, 0, 3).reshape(3, rows, columns)
    return merged[0], merged[1], merged[2]


def solution(mesh):
    row = P(("tm", "inner"), None)
    return jax.shard_map(
        local,
        mesh=mesh,
        in_specs=(row, row, row, row, P(("tm", "inner"))),
        out_specs=(row, row, row),
        check_vma=False,
    )
```

```python
import functools

import jax
import jax.numpy as jnp
from jax import lax
from jax.sharding import PartitionSpec as P

DH = 112

loss_scale = 1024.0


ROW = 8


def shifted(value, count, step):
    total = lax.axis_size("tm")
    pairs = []
    for base in range(0, total, count):
        for i in range(count):
            pairs.append((base + i, base + (i + step) % count))
    return lax.ppermute(value, "tm", pairs)


def strided(value, stride, step):
    total = lax.axis_size("tm")
    rows = total // stride
    pairs = []
    for r in range(rows):
        for j in range(stride):
            pairs.append((r * stride + j, ((r + step) % rows) * stride + j))
    return lax.ppermute(value, "tm", pairs)


def visible(part, label, later):
    total = lax.axis_size("tm")
    row = min(ROW, total)
    rows = total // row
    me = lax.axis_index("tm") // row
    flabel = label.astype(jnp.float32)
    tag = jnp.broadcast_to(flabel, part.shape[:-1] + (1,))
    packed = jnp.concatenate([part, tag], axis=-1)
    frames = [packed] + [shifted(packed, row, s) for s in range(1, row)]
    labels = [f[0, 0, DH + 1] for f in frames]
    states = [f[..., : DH + 1] for f in frames]
    keep = [(l >= flabel) if later else (l <= flabel) for l in labels]
    seen = sum(jnp.where(k, s, 0.0) for k, s in zip(keep, states))
    if rows > 1:
        edge = functools.reduce(jnp.maximum, labels) if later else functools.reduce(jnp.minimum, labels)
        whole = sum(states)
        edge_sum = sum(jnp.where(l == edge, s, 0.0) for l, s in zip(labels, states))
        etag = jnp.broadcast_to(edge, part.shape[:-1] + (1,))
        summary = jnp.stack(
            [jnp.concatenate([whole, etag], -1), jnp.concatenate([edge_sum, etag], -1)]
        )
        for s in range(1, rows):
            got = strided(summary, row, s)
            source = (me - s) % rows
            their_edge = got[1, 0, 0, DH + 1]
            full = (source > me) if later else (source < me)
            part_only = ((source < me) if later else (source > me)) & (their_edge == flabel)
            seen = (
                seen
                + jnp.where(full, got[0, ..., : DH + 1], 0.0)
                + jnp.where(part_only, got[1, ..., : DH + 1], 0.0)
            )
    return seen.astype(jnp.bfloat16)


def local(query_input, key_input, value_input, cotangent, span_labels):
    groups = lax.axis_size("inner")
    rows, columns = query_input.shape
    width = columns // groups
    heads = width // DH
    tokens = rows * groups

    def to_heads(arrays):
        count = len(arrays)
        outgoing = jnp.stack(arrays).reshape(count, rows, groups, width).transpose(2, 0, 1, 3)
        incoming = lax.all_to_all(outgoing, "inner", 0, 0, tiled=True)
        arrived = incoming.transpose(1, 0, 2, 3).reshape(count, tokens, heads, DH)
        return [arrived[i] for i in range(count)]

    def to_rows(arrays):
        count = len(arrays)
        leaving = jnp.stack(arrays).reshape(count, groups, rows, width).transpose(1, 0, 2, 3)
        returned = lax.all_to_all(leaving, "inner", 0, 0, tiled=True)
        merged = returned.transpose(1, 2, 0, 3).reshape(count, rows, columns)
        return [merged[i] for i in range(count)]

    key_heads, value_heads = to_heads([key_input, value_input])
    query_heads, cotangent_heads = to_heads([query_input, cotangent])

    feat_query = jnp.maximum(query_heads, 0)
    feat_key = jnp.maximum(key_heads, 0)
    label = span_labels[0]
    ones = jnp.ones((tokens, heads, 1), jnp.bfloat16)
    value_aug = jnp.concatenate([value_heads, ones], axis=-1)
    state_part = jnp.einsum(
        "thk,thv->hkv", feat_key, value_aug, preferred_element_type=jnp.float32
    )
    state_vis = visible(state_part, label, False)
    both = jnp.einsum("thk,hkv->thv", feat_query, state_vis, preferred_element_type=jnp.float32)
    numerator = both[..., :DH]
    weight = both[..., DH]
    denominator = weight / DH + 1.0
    output = numerator / (DH * denominator[..., None])
    scaled = cotangent_heads.astype(jnp.float32) * loss_scale
    numer_back = (scaled / (DH * denominator[..., None])).astype(jnp.bfloat16)
    weight_back = (-jnp.sum(scaled * output, axis=-1) / (DH * denominator)).astype(jnp.bfloat16)
    back_aug = jnp.concatenate([numer_back, weight_back[..., None]], axis=-1)
    adjoint_part = jnp.einsum(
        "thk,thv->hkv", feat_query, back_aug, preferred_element_type=jnp.float32
    )
    query_feat = jnp.einsum("thv,hkv->thk", back_aug, state_vis, preferred_element_type=jnp.float32)
    query_back = jnp.where(query_heads > 0, query_feat, 0.0).astype(jnp.bfloat16)
    adjoint_vis = visible(adjoint_part, label, True)
    key_feat = jnp.einsum("thv,hkv->thk", value_aug, adjoint_vis, preferred_element_type=jnp.float32)
    value_back = jnp.einsum(
        "thk,hkv->thv", feat_key, adjoint_vis[..., :DH], preferred_element_type=jnp.float32
    )
    key_back = jnp.where(key_heads > 0, key_feat, 0.0).astype(jnp.bfloat16)

    (query_out,) = to_rows([query_back])
    key_out, value_out = to_rows([key_back, value_back.astype(jnp.bfloat16)])
    return query_out, key_out, value_out


def solution(mesh):
    row = P(("tm", "inner"), None)
    return jax.shard_map(
        local,
        mesh=mesh,
        in_specs=(row, row, row, row, P(("tm", "inner"))),
        out_specs=(row, row, row),
        check_vma=False,
    )
```

```python
import functools

import jax
import jax.numpy as jnp
from jax import lax
from jax.sharding import PartitionSpec as P

DH = 112

loss_scale = 1024.0


ROW = 8


def shifted(value, count, step):
    total = lax.axis_size("tm")
    pairs = []
    for base in range(0, total, count):
        for i in range(count):
            pairs.append((base + i, base + (i + step) % count))
    return lax.ppermute(value, "tm", pairs)


def strided(value, stride, step):
    total = lax.axis_size("tm")
    rows = total // stride
    pairs = []
    for r in range(rows):
        for j in range(stride):
            pairs.append((r * stride + j, ((r + step) % rows) * stride + j))
    return lax.ppermute(value, "tm", pairs)


def visible(part, label, later):
    total = lax.axis_size("tm")
    row = min(ROW, total)
    rows = total // row
    me = lax.axis_index("tm") // row
    flabel = label.astype(jnp.float32)
    lanes = 128
    spare = jnp.zeros(part.shape[:-1] + (lanes - DH - 1,), jnp.float32)
    lane = lax.broadcasted_iota(jnp.int32, part.shape[:-1] + (lanes,), 2)
    is_tag = lane == DH + 1
    packed = jnp.where(is_tag, flabel, jnp.concatenate([part, spare], axis=-1))
    frames = [packed] + [shifted(packed, row, s) for s in range(1, row)]
    labels = [f[0, 0, DH + 1] for f in frames]
    keep = [(l >= flabel) if later else (l <= flabel) for l in labels]
    seen = sum(jnp.where(k, f, 0.0) for k, f in zip(keep, frames))
    if rows > 1:
        edge = functools.reduce(jnp.maximum, labels) if later else functools.reduce(jnp.minimum, labels)
        whole = jnp.where(is_tag, edge, sum(frames))
        edge_sum = jnp.where(is_tag, edge, sum(jnp.where(l == edge, f, 0.0) for l, f in zip(labels, frames)))
        summary = jnp.stack([whole, edge_sum])
        for s in range(1, rows):
            got = strided(summary, row, s)
            source = (me - s) % rows
            their_edge = got[1, 0, 0, DH + 1]
            full = (source > me) if later else (source < me)
            part_only = ((source < me) if later else (source > me)) & (their_edge == flabel)
            seen = seen + jnp.where(full, got[0], 0.0) + jnp.where(part_only, got[1], 0.0)
    return seen[..., : DH + 1].astype(jnp.bfloat16)


def local(query_input, key_input, value_input, cotangent, span_labels):
    groups = lax.axis_size("inner")
    rows, columns = query_input.shape
    width = columns // groups
    heads = width // DH
    tokens = rows * groups

    def to_heads(arrays):
        count = len(arrays)
        outgoing = jnp.stack(arrays).reshape(count, rows, groups, width).transpose(2, 0, 1, 3)
        incoming = lax.all_to_all(outgoing, "inner", 0, 0, tiled=True)
        arrived = incoming.transpose(1, 0, 2, 3).reshape(count, tokens, heads, DH)
        return [arrived[i] for i in range(count)]

    def to_rows(arrays):
        count = len(arrays)
        leaving = jnp.stack(arrays).reshape(count, groups, rows, width).transpose(1, 0, 2, 3)
        returned = lax.all_to_all(leaving, "inner", 0, 0, tiled=True)
        merged = returned.transpose(1, 2, 0, 3).reshape(count, rows, columns)
        return [merged[i] for i in range(count)]

    key_heads, value_heads = to_heads([key_input, value_input])
    query_heads, cotangent_heads = to_heads([query_input, cotangent])

    feat_query = jnp.maximum(query_heads, 0)
    feat_key = jnp.maximum(key_heads, 0)
    label = span_labels[0]
    ones = jnp.ones((tokens, heads, 1), jnp.bfloat16)
    value_aug = jnp.concatenate([value_heads, ones], axis=-1)
    state_part = jnp.einsum(
        "thk,thv->hkv", feat_key, value_aug, preferred_element_type=jnp.float32
    )
    state_vis = visible(state_part, label, False)
    both = jnp.einsum("thk,hkv->thv", feat_query, state_vis, preferred_element_type=jnp.float32)
    numerator = both[..., :DH]
    weight = both[..., DH]
    denominator = weight / DH + 1.0
    output = numerator / (DH * denominator[..., None])
    scaled = cotangent_heads.astype(jnp.float32) * loss_scale
    numer_back = (scaled / (DH * denominator[..., None])).astype(jnp.bfloat16)
    weight_back = (-jnp.sum(scaled * output, axis=-1) / (DH * denominator)).astype(jnp.bfloat16)
    back_aug = jnp.concatenate([numer_back, weight_back[..., None]], axis=-1)
    adjoint_part = jnp.einsum(
        "thk,thv->hkv", feat_query, back_aug, preferred_element_type=jnp.float32
    )
    query_feat = jnp.einsum("thv,hkv->thk", back_aug, state_vis, preferred_element_type=jnp.float32)
    query_back = jnp.where(query_heads > 0, query_feat, 0.0).astype(jnp.bfloat16)
    adjoint_vis = visible(adjoint_part, label, True)
    key_feat = jnp.einsum("thv,hkv->thk", value_aug, adjoint_vis, preferred_element_type=jnp.float32)
    value_back = jnp.einsum(
        "thk,hkv->thv", feat_key, adjoint_vis[..., :DH], preferred_element_type=jnp.float32
    )
    key_back = jnp.where(key_heads > 0, key_feat, 0.0).astype(jnp.bfloat16)

    (query_out,) = to_rows([query_back])
    key_out, value_out = to_rows([key_back, value_back.astype(jnp.bfloat16)])
    return query_out, key_out, value_out


def solution(mesh):
    row = P(("tm", "inner"), None)
    return jax.shard_map(
        local,
        mesh=mesh,
        in_specs=(row, row, row, row, P(("tm", "inner"))),
        out_specs=(row, row, row),
        check_vma=False,
    )
```

```python
import jax
import jax.numpy as jnp
from jax import lax
from jax.sharding import PartitionSpec as P

DH = 112

loss_scale = 1024.0


ROW = 8


def shifted(value, count, step):
    total = lax.axis_size("tm")
    pairs = []
    for base in range(0, total, count):
        for i in range(count):
            pairs.append((base + i, base + (i + step) % count))
    return lax.ppermute(value, "tm", pairs)


def strided(value, stride, step):
    total = lax.axis_size("tm")
    rows = total // stride
    pairs = []
    for r in range(rows):
        for j in range(stride):
            pairs.append((r * stride + j, ((r + step) % rows) * stride + j))
    return lax.ppermute(value, "tm", pairs)


def visible(part, label, later):
    total = lax.axis_size("tm")
    row = min(ROW, total)
    rows = total // row
    me = lax.axis_index("tm") // row
    flabel = label.astype(jnp.float32)
    lanes = 128
    spare = jnp.zeros(part.shape[:-1] + (lanes - DH - 1,), jnp.float32)
    lane = lax.broadcasted_iota(jnp.int32, part.shape[:-1] + (lanes,), 2)
    is_tag = lane == DH + 1
    packed = jnp.where(is_tag, flabel, jnp.concatenate([part, spare], axis=-1))
    frames = jnp.stack([packed] + [shifted(packed, row, s) for s in range(1, row)])
    labels = frames[:, 0, 0, DH + 1]
    keep = (labels >= flabel) if later else (labels <= flabel)
    seen = jnp.sum(jnp.where(keep[:, None, None, None], frames, 0.0), axis=0)
    if rows > 1:
        edge = jnp.max(labels) if later else jnp.min(labels)
        whole = jnp.where(is_tag, edge, jnp.sum(frames, axis=0))
        on_edge = (labels == edge)[:, None, None, None]
        edge_sum = jnp.where(is_tag, edge, jnp.sum(jnp.where(on_edge, frames, 0.0), axis=0))
        summary = jnp.stack([whole, edge_sum])
        got = jnp.stack([strided(summary, row, s) for s in range(1, rows)])
        source = (me - jnp.arange(1, rows)) % rows
        their_edge = got[:, 1, 0, 0, DH + 1]
        full = (source > me) if later else (source < me)
        part_only = ((source < me) if later else (source > me)) & (their_edge == flabel)
        seen = seen + jnp.sum(
            jnp.where(full[:, None, None, None], got[:, 0], 0.0)
            + jnp.where(part_only[:, None, None, None], got[:, 1], 0.0),
            axis=0,
        )
    return seen[..., : DH + 1].astype(jnp.bfloat16)


def local(query_input, key_input, value_input, cotangent, span_labels):
    groups = lax.axis_size("inner")
    rows, columns = query_input.shape
    width = columns // groups
    heads = width // DH
    tokens = rows * groups

    def to_heads(arrays):
        count = len(arrays)
        outgoing = jnp.stack(arrays).reshape(count, rows, groups, width).transpose(2, 0, 1, 3)
        incoming = lax.all_to_all(outgoing, "inner", 0, 0, tiled=True)
        arrived = incoming.transpose(1, 0, 2, 3).reshape(count, tokens, heads, DH)
        return [arrived[i] for i in range(count)]

    def to_rows(arrays):
        count = len(arrays)
        leaving = jnp.stack(arrays).reshape(count, groups, rows, width).transpose(1, 0, 2, 3)
        returned = lax.all_to_all(leaving, "inner", 0, 0, tiled=True)
        merged = returned.transpose(1, 2, 0, 3).reshape(count, rows, columns)
        return [merged[i] for i in range(count)]

    key_heads, value_heads = to_heads([key_input, value_input])
    query_heads, cotangent_heads = to_heads([query_input, cotangent])

    feat_query = jnp.maximum(query_heads, 0)
    feat_key = jnp.maximum(key_heads, 0)
    label = span_labels[0]
    ones = jnp.ones((tokens, heads, 1), jnp.bfloat16)
    value_aug = jnp.concatenate([value_heads, ones], axis=-1)
    state_part = jnp.einsum(
        "thk,thv->hkv", feat_key, value_aug, preferred_element_type=jnp.float32
    )
    state_vis = visible(state_part, label, False)
    both = jnp.einsum("thk,hkv->thv", feat_query, state_vis, preferred_element_type=jnp.float32)
    numerator = both[..., :DH]
    weight = both[..., DH]
    denominator = weight / DH + 1.0
    output = numerator / (DH * denominator[..., None])
    scaled = cotangent_heads.astype(jnp.float32) * loss_scale
    numer_back = (scaled / (DH * denominator[..., None])).astype(jnp.bfloat16)
    weight_back = (-jnp.sum(scaled * output, axis=-1) / (DH * denominator)).astype(jnp.bfloat16)
    back_aug = jnp.concatenate([numer_back, weight_back[..., None]], axis=-1)
    adjoint_part = jnp.einsum(
        "thk,thv->hkv", feat_query, back_aug, preferred_element_type=jnp.float32
    )
    query_feat = jnp.einsum("thv,hkv->thk", back_aug, state_vis, preferred_element_type=jnp.float32)
    query_back = jnp.where(query_heads > 0, query_feat, 0.0).astype(jnp.bfloat16)
    adjoint_vis = visible(adjoint_part, label, True)
    key_feat = jnp.einsum("thv,hkv->thk", value_aug, adjoint_vis, preferred_element_type=jnp.float32)
    value_back = jnp.einsum(
        "thk,hkv->thv", feat_key, adjoint_vis[..., :DH], preferred_element_type=jnp.float32
    )
    key_back = jnp.where(key_heads > 0, key_feat, 0.0).astype(jnp.bfloat16)

    (query_out,) = to_rows([query_back])
    key_out, value_out = to_rows([key_back, value_back.astype(jnp.bfloat16)])
    return query_out, key_out, value_out


def solution(mesh):
    row = P(("tm", "inner"), None)
    return jax.shard_map(
        local,
        mesh=mesh,
        in_specs=(row, row, row, row, P(("tm", "inner"))),
        out_specs=(row, row, row),
        check_vma=False,
    )
```

```python
import functools

import jax
import jax.numpy as jnp
from jax import lax
from jax.sharding import PartitionSpec as P

DH = 112

loss_scale = 1024.0


ROW = 8


def shifted(value, count, step):
    total = lax.axis_size("tm")
    pairs = []
    for base in range(0, total, count):
        for i in range(count):
            pairs.append((base + i, base + (i + step) % count))
    return lax.ppermute(value, "tm", pairs)


def strided(value, stride, step):
    total = lax.axis_size("tm")
    rows = total // stride
    pairs = []
    for r in range(rows):
        for j in range(stride):
            pairs.append((r * stride + j, ((r + step) % rows) * stride + j))
    return lax.ppermute(value, "tm", pairs)


def visible(part, label, later):
    total = lax.axis_size("tm")
    row = min(ROW, total)
    rows = total // row
    me = lax.axis_index("tm") // row
    flabel = label.astype(jnp.float32)
    tag = jnp.broadcast_to(flabel, part.shape[:-1] + (1,))
    packed = jnp.concatenate([part, tag], axis=-1)
    frames = [packed] + [shifted(packed, row, s) for s in range(1, row)]
    labels = [f[0, 0, DH + 1] for f in frames]
    states = [f[..., : DH + 1] for f in frames]
    keep = [(l >= flabel) if later else (l <= flabel) for l in labels]
    seen = sum(jnp.where(k, s, 0.0) for k, s in zip(keep, states))
    if rows > 1:
        edge = functools.reduce(jnp.maximum, labels) if later else functools.reduce(jnp.minimum, labels)
        whole = sum(states)
        edge_sum = sum(jnp.where(l == edge, s, 0.0) for l, s in zip(labels, states))
        etag = jnp.broadcast_to(edge, part.shape[:-1] + (1,))
        summary = jnp.stack(
            [jnp.concatenate([whole, etag], -1), jnp.concatenate([edge_sum, etag], -1)]
        )
        for s in range(1, rows):
            got = strided(summary, row, s)
            source = (me - s) % rows
            their_edge = got[1, 0, 0, DH + 1]
            full = (source > me) if later else (source < me)
            part_only = ((source < me) if later else (source > me)) & (their_edge == flabel)
            seen = (
                seen
                + jnp.where(full, got[0, ..., : DH + 1], 0.0)
                + jnp.where(part_only, got[1, ..., : DH + 1], 0.0)
            )
    return seen.astype(jnp.bfloat16)


def local(query_input, key_input, value_input, cotangent, span_labels):
    groups = lax.axis_size("inner")
    rows, columns = query_input.shape
    width = columns // groups
    heads = width // DH
    tokens = rows * groups

    def to_heads(arrays):
        count = len(arrays)
        outgoing = jnp.stack(arrays).reshape(count, rows, groups, width).transpose(2, 0, 1, 3)
        incoming = lax.all_to_all(outgoing, "inner", 0, 0, tiled=True)
        arrived = incoming.transpose(1, 0, 2, 3).reshape(count, tokens, heads, DH)
        return [arrived[i] for i in range(count)]

    def to_rows(arrays):
        count = len(arrays)
        leaving = jnp.stack(arrays).reshape(count, groups, rows, width).transpose(1, 0, 2, 3)
        returned = lax.all_to_all(leaving, "inner", 0, 0, tiled=True)
        merged = returned.transpose(1, 2, 0, 3).reshape(count, rows, columns)
        return [merged[i] for i in range(count)]

    key_heads, value_heads = to_heads([key_input, value_input])
    query_heads, cotangent_heads = to_heads([query_input, cotangent])

    feat_query = jnp.maximum(query_heads, 0)
    feat_key = jnp.maximum(key_heads, 0)
    label = span_labels[0]
    ones = jnp.ones((tokens, heads, 1), jnp.bfloat16)
    value_aug = jnp.concatenate([value_heads, ones], axis=-1)
    state_part = jnp.einsum(
        "thk,thv->hkv", feat_key, value_aug, preferred_element_type=jnp.float32
    )
    state_vis = visible(state_part, label, False)
    both = jnp.einsum("thk,hkv->thv", feat_query, state_vis, preferred_element_type=jnp.float32)
    numerator = both[..., :DH]
    weight = both[..., DH]
    denominator = weight / DH + 1.0
    output = numerator / (DH * denominator[..., None])
    scaled = cotangent_heads.astype(jnp.float32) * loss_scale
    numer_back = (scaled / (DH * denominator[..., None])).astype(jnp.bfloat16)
    weight_back = (-jnp.sum(scaled * output, axis=-1) / (DH * denominator)).astype(jnp.bfloat16)
    back_aug = jnp.concatenate([numer_back, weight_back[..., None]], axis=-1)
    adjoint_part = jnp.einsum(
        "thk,thv->hkv", feat_query, back_aug, preferred_element_type=jnp.float32
    )
    query_feat = jnp.einsum("thv,hkv->thk", back_aug, state_vis, preferred_element_type=jnp.float32)
    query_back = jnp.where(query_heads > 0, query_feat, 0.0).astype(jnp.bfloat16)
    adjoint_vis = visible(adjoint_part, label, True)
    (query_out,) = to_rows([query_back])

    copies = jnp.broadcast_to(adjoint_vis[None], (groups,) + adjoint_vis.shape)
    adjoint_all = lax.all_to_all(copies, "inner", 0, 0, tiled=True).reshape(
        groups * heads, DH, DH + 1
    )
    all_heads = groups * heads
    own_key = key_input.reshape(rows, all_heads, DH)
    own_value = value_input.reshape(rows, all_heads, DH)
    own_feat_key = jnp.maximum(own_key, 0)
    key_feat = jnp.einsum(
        "thv,hkv->thk", own_value, adjoint_all[..., :DH], preferred_element_type=jnp.float32
    ) + adjoint_all[..., DH].astype(jnp.float32)[None]
    value_back = jnp.einsum(
        "thk,hkv->thv", own_feat_key, adjoint_all[..., :DH], preferred_element_type=jnp.float32
    )
    key_out = jnp.where(own_key > 0, key_feat, 0.0).astype(jnp.bfloat16).reshape(rows, columns)
    value_out = value_back.astype(jnp.bfloat16).reshape(rows, columns)
    return query_out, key_out, value_out


def solution(mesh):
    row = P(("tm", "inner"), None)
    return jax.shard_map(
        local,
        mesh=mesh,
        in_specs=(row, row, row, row, P(("tm", "inner"))),
        out_specs=(row, row, row),
        check_vma=False,
    )
```

```python
import jax
import jax.numpy as jnp
from jax import lax
from jax.sharding import PartitionSpec as P

DH = 112

loss_scale = 1024.0


ROW = 8


def shifted(value, count, step):
    total = lax.axis_size("tm")
    pairs = []
    for base in range(0, total, count):
        for i in range(count):
            pairs.append((base + i, base + (i + step) % count))
    return lax.ppermute(value, "tm", pairs)


def strided(value, stride, step):
    total = lax.axis_size("tm")
    rows = total // stride
    pairs = []
    for r in range(rows):
        for j in range(stride):
            pairs.append((r * stride + j, ((r + step) % rows) * stride + j))
    return lax.ppermute(value, "tm", pairs)


def visible(part, label, later):
    total = lax.axis_size("tm")
    row = min(ROW, total)
    rows = total // row
    me = lax.axis_index("tm") // row
    flabel = label.astype(jnp.float32)
    tag = jnp.broadcast_to(flabel, part.shape[:-1] + (1,))
    packed = jnp.concatenate([part, tag], axis=-1)
    frames = [packed] + [shifted(packed, row, s) for s in range(1, row)]
    tags = [f[..., DH + 1 :] for f in frames]
    states = [f[..., : DH + 1] for f in frames]
    keep = [(t >= flabel) if later else (t <= flabel) for t in tags]
    seen = sum(jnp.where(k, s, 0.0) for k, s in zip(keep, states))
    if rows > 1:
        pick = jnp.maximum if later else jnp.minimum
        edge = tags[0]
        for t in tags[1:]:
            edge = pick(edge, t)
        whole = sum(states)
        edge_sum = sum(jnp.where(t == edge, s, 0.0) for t, s in zip(tags, states))
        summary = jnp.stack(
            [jnp.concatenate([whole, edge], -1), jnp.concatenate([edge_sum, edge], -1)]
        )
        for s in range(1, rows):
            got = strided(summary, row, s)
            source = (me - s) % rows
            their_edge = got[1, ..., DH + 1 :]
            full = (source > me) if later else (source < me)
            part_only = ((source < me) if later else (source > me)) & (their_edge == flabel)
            seen = (
                seen
                + jnp.where(full, got[0, ..., : DH + 1], 0.0)
                + jnp.where(part_only, got[1, ..., : DH + 1], 0.0)
            )
    return seen.astype(jnp.bfloat16)


def local(query_input, key_input, value_input, cotangent, span_labels):
    groups = lax.axis_size("inner")
    rows, columns = query_input.shape
    width = columns // groups
    heads = width // DH
    tokens = rows * groups

    def to_heads(arrays):
        count = len(arrays)
        outgoing = jnp.stack(arrays).reshape(count, rows, groups, width).transpose(2, 0, 1, 3)
        incoming = lax.all_to_all(outgoing, "inner", 0, 0, tiled=True)
        arrived = incoming.transpose(1, 0, 2, 3).reshape(count, tokens, heads, DH)
        return [arrived[i] for i in range(count)]

    def to_rows(arrays):
        count = len(arrays)
        leaving = jnp.stack(arrays).reshape(count, groups, rows, width).transpose(1, 0, 2, 3)
        returned = lax.all_to_all(leaving, "inner", 0, 0, tiled=True)
        merged = returned.transpose(1, 2, 0, 3).reshape(count, rows, columns)
        return [merged[i] for i in range(count)]

    key_heads, value_heads = to_heads([key_input, value_input])
    query_heads, cotangent_heads = to_heads([query_input, cotangent])

    feat_query = jnp.maximum(query_heads, 0)
    feat_key = jnp.maximum(key_heads, 0)
    label = span_labels[0]
    ones = jnp.ones((tokens, heads, 1), jnp.bfloat16)
    value_aug = jnp.concatenate([value_heads, ones], axis=-1)
    state_part = jnp.einsum(
        "thk,thv->hkv", feat_key, value_aug, preferred_element_type=jnp.float32
    )
    state_vis = visible(state_part, label, False)
    both = jnp.einsum("thk,hkv->thv", feat_query, state_vis, preferred_element_type=jnp.float32)
    numerator = both[..., :DH]
    weight = both[..., DH]
    denominator = weight / DH + 1.0
    output = numerator / (DH * denominator[..., None])
    scaled = cotangent_heads.astype(jnp.float32) * loss_scale
    numer_back = (scaled / (DH * denominator[..., None])).astype(jnp.bfloat16)
    weight_back = (-jnp.sum(scaled * output, axis=-1) / (DH * denominator)).astype(jnp.bfloat16)
    back_aug = jnp.concatenate([numer_back, weight_back[..., None]], axis=-1)
    adjoint_part = jnp.einsum(
        "thk,thv->hkv", feat_query, back_aug, preferred_element_type=jnp.float32
    )
    query_feat = jnp.einsum("thv,hkv->thk", back_aug, state_vis, preferred_element_type=jnp.float32)
    query_back = jnp.where(query_heads > 0, query_feat, 0.0).astype(jnp.bfloat16)
    adjoint_vis = visible(adjoint_part, label, True)
    (query_out,) = to_rows([query_back])

    copies = jnp.broadcast_to(adjoint_vis[None], (groups,) + adjoint_vis.shape)
    adjoint_all = lax.all_to_all(copies, "inner", 0, 0, tiled=True).reshape(
        groups * heads, DH, DH + 1
    )
    all_heads = groups * heads
    own_key = key_input.reshape(rows, all_heads, DH)
    own_value = value_input.reshape(rows, all_heads, DH)
    own_feat_key = jnp.maximum(own_key, 0)
    key_feat = jnp.einsum(
        "thv,hkv->thk", own_value, adjoint_all[..., :DH], preferred_element_type=jnp.float32
    ) + adjoint_all[..., DH].astype(jnp.float32)[None]
    value_back = jnp.einsum(
        "thk,hkv->thv", own_feat_key, adjoint_all[..., :DH], preferred_element_type=jnp.float32
    )
    key_out = jnp.where(own_key > 0, key_feat, 0.0).astype(jnp.bfloat16).reshape(rows, columns)
    value_out = value_back.astype(jnp.bfloat16).reshape(rows, columns)
    return query_out, key_out, value_out


def solution(mesh):
    row = P(("tm", "inner"), None)
    return jax.shard_map(
        local,
        mesh=mesh,
        in_specs=(row, row, row, row, P(("tm", "inner"))),
        out_specs=(row, row, row),
        check_vma=False,
    )
```

```python
import jax
import jax.numpy as jnp
from jax import lax
from jax.sharding import PartitionSpec as P

DH = 112

loss_scale = 1024.0


ROW = 8


def shifted(value, count, step):
    total = lax.axis_size("tm")
    pairs = []
    for base in range(0, total, count):
        for i in range(count):
            pairs.append((base + i, base + (i + step) % count))
    return lax.ppermute(value, "tm", pairs)


def strided(value, stride, step):
    total = lax.axis_size("tm")
    rows = total // stride
    pairs = []
    for r in range(rows):
        for j in range(stride):
            pairs.append((r * stride + j, ((r + step) % rows) * stride + j))
    return lax.ppermute(value, "tm", pairs)


def visible(part, label, later):
    total = lax.axis_size("tm")
    row = min(ROW, total)
    rows = total // row
    me = lax.axis_index("tm") // row
    flabel = label.astype(jnp.float32)
    tag = jnp.broadcast_to(flabel, part.shape[:-1] + (1,))
    packed = jnp.concatenate([part, tag], axis=-1)
    in_row = [list(range(base, base + row)) for base in range(0, total, row)]
    frames = lax.all_to_all(
        jnp.broadcast_to(packed[None], (row,) + packed.shape),
        "tm", 0, 0, tiled=True, axis_index_groups=in_row,
    )
    tags = frames[..., DH + 1 :]
    states = frames[..., : DH + 1]
    keep = (tags >= flabel) if later else (tags <= flabel)
    seen = jnp.sum(jnp.where(keep, states, 0.0), axis=0)
    if rows > 1:
        edge = jnp.max(tags, axis=0) if later else jnp.min(tags, axis=0)
        whole = jnp.sum(states, axis=0)
        edge_sum = jnp.sum(jnp.where(tags == edge[None], states, 0.0), axis=0)
        summary = jnp.stack(
            [jnp.concatenate([whole, edge], -1), jnp.concatenate([edge_sum, edge], -1)]
        )
        across = [list(range(j, total, row)) for j in range(row)]
        got = lax.all_to_all(
            jnp.broadcast_to(summary[None], (rows,) + summary.shape),
            "tm", 0, 0, tiled=True, axis_index_groups=across,
        )
        source = jnp.arange(rows).reshape(rows, 1, 1, 1)
        their_edge = got[:, 1, ..., DH + 1 :]
        full = (source > me) if later else (source < me)
        part_only = ((source < me) if later else (source > me)) & (their_edge == flabel)
        seen = seen + jnp.sum(
            jnp.where(full, got[:, 0, ..., : DH + 1], 0.0)
            + jnp.where(part_only, got[:, 1, ..., : DH + 1], 0.0),
            axis=0,
        )
    return seen.astype(jnp.bfloat16)


def local(query_input, key_input, value_input, cotangent, span_labels):
    groups = lax.axis_size("inner")
    rows, columns = query_input.shape
    width = columns // groups
    heads = width // DH
    tokens = rows * groups

    def to_heads(arrays):
        count = len(arrays)
        outgoing = jnp.stack(arrays).reshape(count, rows, groups, width).transpose(2, 0, 1, 3)
        incoming = lax.all_to_all(outgoing, "inner", 0, 0, tiled=True)
        arrived = incoming.transpose(1, 0, 2, 3).reshape(count, tokens, heads, DH)
        return [arrived[i] for i in range(count)]

    def to_rows(arrays):
        count = len(arrays)
        leaving = jnp.stack(arrays).reshape(count, groups, rows, width).transpose(1, 0, 2, 3)
        returned = lax.all_to_all(leaving, "inner", 0, 0, tiled=True)
        merged = returned.transpose(1, 2, 0, 3).reshape(count, rows, columns)
        return [merged[i] for i in range(count)]

    key_heads, value_heads = to_heads([key_input, value_input])
    query_heads, cotangent_heads = to_heads([query_input, cotangent])

    feat_query = jnp.maximum(query_heads, 0)
    feat_key = jnp.maximum(key_heads, 0)
    label = span_labels[0]
    ones = jnp.ones((tokens, heads, 1), jnp.bfloat16)
    value_aug = jnp.concatenate([value_heads, ones], axis=-1)
    state_part = jnp.einsum(
        "thk,thv->hkv", feat_key, value_aug, preferred_element_type=jnp.float32
    )
    state_vis = visible(state_part, label, False)
    both = jnp.einsum("thk,hkv->thv", feat_query, state_vis, preferred_element_type=jnp.float32)
    numerator = both[..., :DH]
    weight = both[..., DH]
    denominator = weight / DH + 1.0
    output = numerator / (DH * denominator[..., None])
    scaled = cotangent_heads.astype(jnp.float32) * loss_scale
    numer_back = (scaled / (DH * denominator[..., None])).astype(jnp.bfloat16)
    weight_back = (-jnp.sum(scaled * output, axis=-1) / (DH * denominator)).astype(jnp.bfloat16)
    back_aug = jnp.concatenate([numer_back, weight_back[..., None]], axis=-1)
    adjoint_part = jnp.einsum(
        "thk,thv->hkv", feat_query, back_aug, preferred_element_type=jnp.float32
    )
    query_feat = jnp.einsum("thv,hkv->thk", back_aug, state_vis, preferred_element_type=jnp.float32)
    query_back = jnp.where(query_heads > 0, query_feat, 0.0).astype(jnp.bfloat16)
    adjoint_vis = visible(adjoint_part, label, True)
    (query_out,) = to_rows([query_back])

    copies = jnp.broadcast_to(adjoint_vis[None], (groups,) + adjoint_vis.shape)
    adjoint_all = lax.all_to_all(copies, "inner", 0, 0, tiled=True).reshape(
        groups * heads, DH, DH + 1
    )
    all_heads = groups * heads
    own_key = key_input.reshape(rows, all_heads, DH)
    own_value = value_input.reshape(rows, all_heads, DH)
    own_feat_key = jnp.maximum(own_key, 0)
    key_feat = jnp.einsum(
        "thv,hkv->thk", own_value, adjoint_all[..., :DH], preferred_element_type=jnp.float32
    ) + adjoint_all[..., DH].astype(jnp.float32)[None]
    value_back = jnp.einsum(
        "thk,hkv->thv", own_feat_key, adjoint_all[..., :DH], preferred_element_type=jnp.float32
    )
    key_out = jnp.where(own_key > 0, key_feat, 0.0).astype(jnp.bfloat16).reshape(rows, columns)
    value_out = value_back.astype(jnp.bfloat16).reshape(rows, columns)
    return query_out, key_out, value_out


def solution(mesh):
    row = P(("tm", "inner"), None)
    return jax.shard_map(
        local,
        mesh=mesh,
        in_specs=(row, row, row, row, P(("tm", "inner"))),
        out_specs=(row, row, row),
        check_vma=False,
    )
```

```python
import jax
import jax.numpy as jnp
from jax import lax
from jax.sharding import PartitionSpec as P

DH = 112

loss_scale = 1024.0


ROW = 8


def shifted(value, count, step):
    total = lax.axis_size("tm")
    pairs = []
    for base in range(0, total, count):
        for i in range(count):
            pairs.append((base + i, base + (i + step) % count))
    return lax.ppermute(value, "tm", pairs)


def strided(value, stride, step):
    total = lax.axis_size("tm")
    rows = total // stride
    pairs = []
    for r in range(rows):
        for j in range(stride):
            pairs.append((r * stride + j, ((r + step) % rows) * stride + j))
    return lax.ppermute(value, "tm", pairs)


def visible(part, label, later):
    total = lax.axis_size("tm")
    row = min(ROW, total)
    rows = total // row
    me = lax.axis_index("tm") // row
    flabel = label.astype(jnp.float32)
    tag = jnp.broadcast_to(flabel, part.shape[:-1] + (1,))
    packed = jnp.concatenate([part, tag], axis=-1)
    frames = [packed] + [shifted(packed, row, s) for s in range(1, row)]
    tags = [f[..., DH + 1 :] for f in frames]
    states = [f[..., : DH + 1] for f in frames]
    keep = [(t >= flabel) if later else (t <= flabel) for t in tags]
    seen = sum(jnp.where(k, s, 0.0) for k, s in zip(keep, states))
    if rows > 1:
        pick = jnp.maximum if later else jnp.minimum
        edge = tags[0]
        for t in tags[1:]:
            edge = pick(edge, t)
        whole = sum(states)
        edge_sum = sum(jnp.where(t == edge, s, 0.0) for t, s in zip(tags, states))
        summary = jnp.stack(
            [jnp.concatenate([whole, edge], -1), jnp.concatenate([edge_sum, edge], -1)]
        )
        for s in range(1, rows):
            got = strided(summary, row, s)
            source = (me - s) % rows
            their_edge = got[1, ..., DH + 1 :]
            full = (source > me) if later else (source < me)
            part_only = ((source < me) if later else (source > me)) & (their_edge == flabel)
            seen = (
                seen
                + jnp.where(full, got[0, ..., : DH + 1], 0.0)
                + jnp.where(part_only, got[1, ..., : DH + 1], 0.0)
            )
    return seen.astype(jnp.bfloat16)


def local(query_input, key_input, value_input, cotangent, span_labels):
    groups = lax.axis_size("inner")
    rows, columns = query_input.shape
    width = columns // groups
    heads = width // DH
    tokens = rows * groups

    def to_heads(arrays):
        count = len(arrays)
        outgoing = jnp.stack(arrays).reshape(count, rows, groups, width).transpose(2, 0, 1, 3)
        incoming = lax.all_to_all(outgoing, "inner", 0, 0, tiled=True)
        arrived = incoming.transpose(1, 0, 2, 3).reshape(count, tokens, heads, DH)
        return [arrived[i] for i in range(count)]

    def to_rows(arrays):
        count = len(arrays)
        leaving = jnp.stack(arrays).reshape(count, groups, rows, width).transpose(1, 0, 2, 3)
        returned = lax.all_to_all(leaving, "inner", 0, 0, tiled=True)
        merged = returned.transpose(1, 2, 0, 3).reshape(count, rows, columns)
        return [merged[i] for i in range(count)]

    all_heads = groups * heads
    own_key = key_input.reshape(rows, all_heads, DH)
    own_value = value_input.reshape(rows, all_heads, DH)
    own_feat_key = jnp.maximum(own_key, 0)
    own_ones = jnp.ones((rows, all_heads, 1), jnp.bfloat16)
    own_state = jnp.einsum(
        "thk,thv->hkv",
        own_feat_key,
        jnp.concatenate([own_value, own_ones], axis=-1),
        preferred_element_type=jnp.float32,
    )
    pieces = own_state.astype(jnp.bfloat16).reshape(groups, heads, DH, DH + 1)
    state_part = jnp.sum(
        lax.all_to_all(pieces, "inner", 0, 0, tiled=True).astype(jnp.float32), axis=0
    )
    query_heads, cotangent_heads = to_heads([query_input, cotangent])

    feat_query = jnp.maximum(query_heads, 0)
    label = span_labels[0]
    state_vis = visible(state_part, label, False)
    both = jnp.einsum("thk,hkv->thv", feat_query, state_vis, preferred_element_type=jnp.float32)
    numerator = both[..., :DH]
    weight = both[..., DH]
    denominator = weight / DH + 1.0
    output = numerator / (DH * denominator[..., None])
    scaled = cotangent_heads.astype(jnp.float32) * loss_scale
    numer_back = (scaled / (DH * denominator[..., None])).astype(jnp.bfloat16)
    weight_back = (-jnp.sum(scaled * output, axis=-1) / (DH * denominator)).astype(jnp.bfloat16)
    back_aug = jnp.concatenate([numer_back, weight_back[..., None]], axis=-1)
    adjoint_part = jnp.einsum(
        "thk,thv->hkv", feat_query, back_aug, preferred_element_type=jnp.float32
    )
    query_feat = jnp.einsum("thv,hkv->thk", back_aug, state_vis, preferred_element_type=jnp.float32)
    query_back = jnp.where(query_heads > 0, query_feat, 0.0).astype(jnp.bfloat16)
    adjoint_vis = visible(adjoint_part, label, True)
    (query_out,) = to_rows([query_back])

    copies = jnp.broadcast_to(adjoint_vis[None], (groups,) + adjoint_vis.shape)
    adjoint_all = lax.all_to_all(copies, "inner", 0, 0, tiled=True).reshape(
        groups * heads, DH, DH + 1
    )
    key_feat = jnp.einsum(
        "thv,hkv->thk", own_value, adjoint_all[..., :DH], preferred_element_type=jnp.float32
    ) + adjoint_all[..., DH].astype(jnp.float32)[None]
    value_back = jnp.einsum(
        "thk,hkv->thv", own_feat_key, adjoint_all[..., :DH], preferred_element_type=jnp.float32
    )
    key_out = jnp.where(own_key > 0, key_feat, 0.0).astype(jnp.bfloat16).reshape(rows, columns)
    value_out = value_back.astype(jnp.bfloat16).reshape(rows, columns)
    return query_out, key_out, value_out


def solution(mesh):
    row = P(("tm", "inner"), None)
    return jax.shard_map(
        local,
        mesh=mesh,
        in_specs=(row, row, row, row, P(("tm", "inner"))),
        out_specs=(row, row, row),
        check_vma=False,
    )
```

```python
import jax
import jax.numpy as jnp
from jax import lax
from jax.sharding import PartitionSpec as P

DH = 112

loss_scale = 1024.0


ROW = 8


def shifted(value, count, step):
    total = lax.axis_size("tm")
    pairs = []
    for base in range(0, total, count):
        for i in range(count):
            pairs.append((base + i, base + (i + step) % count))
    return lax.ppermute(value, "tm", pairs)


def strided(value, stride, step):
    total = lax.axis_size("tm")
    rows = total // stride
    pairs = []
    for r in range(rows):
        for j in range(stride):
            pairs.append((r * stride + j, ((r + step) % rows) * stride + j))
    return lax.ppermute(value, "tm", pairs)


def visible(part, label, later):
    total = lax.axis_size("tm")
    row = min(ROW, total)
    rows = total // row
    me = lax.axis_index("tm") // row
    flabel = label.astype(jnp.float32)
    tag = jnp.broadcast_to(flabel, part.shape[:-1] + (1,))
    packed = jnp.concatenate([part, tag], axis=-1)
    frames = [packed] + [shifted(packed, row, s) for s in range(1, row)]
    tags = [f[..., DH + 1 :] for f in frames]
    states = [f[..., : DH + 1] for f in frames]
    keep = [(t >= flabel) if later else (t <= flabel) for t in tags]
    seen = sum(jnp.where(k, s, 0.0) for k, s in zip(keep, states))
    if rows > 1:
        pick = jnp.maximum if later else jnp.minimum
        edge = tags[0]
        for t in tags[1:]:
            edge = pick(edge, t)
        whole = sum(states)
        edge_sum = sum(jnp.where(t == edge, s, 0.0) for t, s in zip(tags, states))
        whole = jnp.concatenate([whole, edge], -1)
        edge_sum = jnp.concatenate([edge_sum, edge], -1)
        for s in range(1, rows):
            target = (me + s) % rows
            sends_whole = (target < me) if later else (target > me)
            got = strided(jnp.where(sends_whole, whole, edge_sum), row, s)
            source = (me - s) % rows
            is_whole = (source > me) if later else (source < me)
            take = is_whole | (got[..., DH + 1 :] == flabel)
            seen = seen + jnp.where(take, got[..., : DH + 1], 0.0)
    return seen.astype(jnp.bfloat16)


def local(query_input, key_input, value_input, cotangent, span_labels):
    groups = lax.axis_size("inner")
    rows, columns = query_input.shape
    width = columns // groups
    heads = width // DH
    tokens = rows * groups

    def to_heads(arrays):
        count = len(arrays)
        outgoing = jnp.stack(arrays).reshape(count, rows, groups, width).transpose(2, 0, 1, 3)
        incoming = lax.all_to_all(outgoing, "inner", 0, 0, tiled=True)
        arrived = incoming.transpose(1, 0, 2, 3).reshape(count, tokens, heads, DH)
        return [arrived[i] for i in range(count)]

    def to_rows(arrays):
        count = len(arrays)
        leaving = jnp.stack(arrays).reshape(count, groups, rows, width).transpose(1, 0, 2, 3)
        returned = lax.all_to_all(leaving, "inner", 0, 0, tiled=True)
        merged = returned.transpose(1, 2, 0, 3).reshape(count, rows, columns)
        return [merged[i] for i in range(count)]

    all_heads = groups * heads
    own_key = key_input.reshape(rows, all_heads, DH)
    own_value = value_input.reshape(rows, all_heads, DH)
    own_feat_key = jnp.maximum(own_key, 0)
    own_ones = jnp.ones((rows, all_heads, 1), jnp.bfloat16)
    own_state = jnp.einsum(
        "thk,thv->hkv",
        own_feat_key,
        jnp.concatenate([own_value, own_ones], axis=-1),
        preferred_element_type=jnp.float32,
    )
    pieces = own_state.astype(jnp.bfloat16).reshape(groups, heads, DH, DH + 1)
    state_part = jnp.sum(
        lax.all_to_all(pieces, "inner", 0, 0, tiled=True).astype(jnp.float32), axis=0
    )
    query_heads, cotangent_heads = to_heads([query_input, cotangent])

    feat_query = jnp.maximum(query_heads, 0)
    label = span_labels[0]
    state_vis = visible(state_part, label, False)
    both = jnp.einsum("thk,hkv->thv", feat_query, state_vis, preferred_element_type=jnp.float32)
    numerator = both[..., :DH]
    weight = both[..., DH]
    denominator = weight / DH + 1.0
    output = numerator / (DH * denominator[..., None])
    scaled = cotangent_heads.astype(jnp.float32) * loss_scale
    numer_back = (scaled / (DH * denominator[..., None])).astype(jnp.bfloat16)
    weight_back = (-jnp.sum(scaled * output, axis=-1) / (DH * denominator)).astype(jnp.bfloat16)
    back_aug = jnp.concatenate([numer_back, weight_back[..., None]], axis=-1)
    adjoint_part = jnp.einsum(
        "thk,thv->hkv", feat_query, back_aug, preferred_element_type=jnp.float32
    )
    query_feat = jnp.einsum("thv,hkv->thk", back_aug, state_vis, preferred_element_type=jnp.float32)
    query_back = jnp.where(query_heads > 0, query_feat, 0.0).astype(jnp.bfloat16)
    adjoint_vis = visible(adjoint_part, label, True)
    (query_out,) = to_rows([query_back])

    copies = jnp.broadcast_to(adjoint_vis[None], (groups,) + adjoint_vis.shape)
    adjoint_all = lax.all_to_all(copies, "inner", 0, 0, tiled=True).reshape(
        groups * heads, DH, DH + 1
    )
    key_feat = jnp.einsum(
        "thv,hkv->thk", own_value, adjoint_all[..., :DH], preferred_element_type=jnp.float32
    ) + adjoint_all[..., DH].astype(jnp.float32)[None]
    value_back = jnp.einsum(
        "thk,hkv->thv", own_feat_key, adjoint_all[..., :DH], preferred_element_type=jnp.float32
    )
    key_out = jnp.where(own_key > 0, key_feat, 0.0).astype(jnp.bfloat16).reshape(rows, columns)
    value_out = value_back.astype(jnp.bfloat16).reshape(rows, columns)
    return query_out, key_out, value_out


def solution(mesh):
    row = P(("tm", "inner"), None)
    return jax.shard_map(
        local,
        mesh=mesh,
        in_specs=(row, row, row, row, P(("tm", "inner"))),
        out_specs=(row, row, row),
        check_vma=False,
    )
```

```python
import jax
import jax.numpy as jnp
from jax import lax
from jax.sharding import PartitionSpec as P

DH = 112

loss_scale = 1024.0


ROW = 8


def shifted(value, count, step):
    total = lax.axis_size("tm")
    pairs = []
    for base in range(0, total, count):
        for i in range(count):
            pairs.append((base + i, base + (i + step) % count))
    return lax.ppermute(value, "tm", pairs)


def strided(value, stride, step):
    total = lax.axis_size("tm")
    rows = total // stride
    pairs = []
    for r in range(rows):
        for j in range(stride):
            pairs.append((r * stride + j, ((r + step) % rows) * stride + j))
    return lax.ppermute(value, "tm", pairs)


def visible(part, label, later):
    total = lax.axis_size("tm")
    row = min(ROW, total)
    rows = total // row
    me = lax.axis_index("tm") // row
    flabel = label.astype(jnp.float32)
    tag = jnp.broadcast_to(flabel, part.shape[:-1] + (1,))
    packed = jnp.concatenate([part, tag], axis=-1)
    frames = [packed] + [shifted(packed, row, s) for s in range(1, row)]
    tags = [f[..., DH + 1 :] for f in frames]
    states = [f[..., : DH + 1] for f in frames]
    keep = [(t >= flabel) if later else (t <= flabel) for t in tags]
    seen = sum(jnp.where(k, s, 0.0) for k, s in zip(keep, states))
    if rows > 1:
        pick = jnp.maximum if later else jnp.minimum
        edge = tags[0]
        for t in tags[1:]:
            edge = pick(edge, t)
        whole = sum(states)
        edge_sum = sum(jnp.where(t == edge, s, 0.0) for t, s in zip(tags, states))
        whole = jnp.concatenate([whole, edge], -1)
        edge_sum = jnp.concatenate([edge_sum, edge], -1)
        for s in range(1, rows):
            target = (me + s) % rows
            sends_whole = (target < me) if later else (target > me)
            got = strided(jnp.where(sends_whole, whole, edge_sum), row, s)
            source = (me - s) % rows
            is_whole = (source > me) if later else (source < me)
            take = is_whole | (got[..., DH + 1 :] == flabel)
            seen = seen + jnp.where(take, got[..., : DH + 1], 0.0)
    return seen.astype(jnp.bfloat16)


def local(query_input, key_input, value_input, cotangent, span_labels):
    groups = lax.axis_size("inner")
    rows, columns = query_input.shape
    width = columns // groups
    heads = width // DH
    tokens = rows * groups

    def to_heads(arrays):
        count = len(arrays)
        outgoing = jnp.stack(arrays).reshape(count, rows, groups, width).transpose(2, 0, 1, 3)
        incoming = lax.all_to_all(outgoing, "inner", 0, 0, tiled=True)
        arrived = incoming.transpose(1, 0, 2, 3).reshape(count, tokens, heads, DH)
        return [arrived[i] for i in range(count)]

    def to_rows(arrays):
        count = len(arrays)
        leaving = jnp.stack(arrays).reshape(count, groups, rows, width).transpose(1, 0, 2, 3)
        returned = lax.all_to_all(leaving, "inner", 0, 0, tiled=True)
        merged = returned.transpose(1, 2, 0, 3).reshape(count, rows, columns)
        return [merged[i] for i in range(count)]

    all_heads = groups * heads
    own_key = key_input.reshape(rows, all_heads, DH)
    own_value = value_input.reshape(rows, all_heads, DH)
    own_feat_key = jnp.maximum(own_key, 0)
    own_ones = jnp.ones((rows, all_heads, 1), jnp.bfloat16)
    own_state = jnp.einsum(
        "thk,thv->hkv",
        own_feat_key,
        jnp.concatenate([own_value, own_ones], axis=-1),
        preferred_element_type=jnp.float32,
    )
    pieces = own_state.astype(jnp.bfloat16).reshape(groups, heads, DH, DH + 1)
    state_part = jnp.sum(
        lax.all_to_all(pieces, "inner", 0, 0, tiled=True).astype(jnp.float32), axis=0
    )
    feat_query, scaled_heads = to_heads(
        [jnp.maximum(query_input, 0), cotangent * jnp.asarray(loss_scale, jnp.bfloat16)]
    )

    label = span_labels[0]
    state_vis = visible(state_part, label, False)
    both = jnp.einsum("thk,hkv->thv", feat_query, state_vis, preferred_element_type=jnp.float32)
    numerator = both[..., :DH]
    weight = both[..., DH]
    denominator = weight / DH + 1.0
    output = numerator / (DH * denominator[..., None])
    scaled = scaled_heads.astype(jnp.float32)
    numer_back = (scaled / (DH * denominator[..., None])).astype(jnp.bfloat16)
    weight_back = (-jnp.sum(scaled * output, axis=-1) / (DH * denominator)).astype(jnp.bfloat16)
    back_aug = jnp.concatenate([numer_back, weight_back[..., None]], axis=-1)
    adjoint_part = jnp.einsum(
        "thk,thv->hkv", feat_query, back_aug, preferred_element_type=jnp.float32
    )
    query_feat = jnp.einsum("thv,hkv->thk", back_aug, state_vis, preferred_element_type=jnp.float32)
    query_back = jnp.where(feat_query > 0, query_feat, 0.0).astype(jnp.bfloat16)
    adjoint_vis = visible(adjoint_part, label, True)
    (query_out,) = to_rows([query_back])

    copies = jnp.broadcast_to(adjoint_vis[None], (groups,) + adjoint_vis.shape)
    adjoint_all = lax.all_to_all(copies, "inner", 0, 0, tiled=True).reshape(
        groups * heads, DH, DH + 1
    )
    key_feat = jnp.einsum(
        "thv,hkv->thk", own_value, adjoint_all[..., :DH], preferred_element_type=jnp.float32
    ) + adjoint_all[..., DH].astype(jnp.float32)[None]
    value_back = jnp.einsum(
        "thk,hkv->thv", own_feat_key, adjoint_all[..., :DH], preferred_element_type=jnp.float32
    )
    key_out = jnp.where(own_key > 0, key_feat, 0.0).astype(jnp.bfloat16).reshape(rows, columns)
    value_out = value_back.astype(jnp.bfloat16).reshape(rows, columns)
    return query_out, key_out, value_out


def solution(mesh):
    row = P(("tm", "inner"), None)
    return jax.shard_map(
        local,
        mesh=mesh,
        in_specs=(row, row, row, row, P(("tm", "inner"))),
        out_specs=(row, row, row),
        check_vma=False,
    )
```

```python
import jax
import jax.numpy as jnp
from jax import lax
from jax.sharding import PartitionSpec as P

DH = 112

loss_scale = 1024.0


ROW = 8


def shifted(value, count, step):
    total = lax.axis_size("tm")
    pairs = []
    for base in range(0, total, count):
        for i in range(count):
            pairs.append((base + i, base + (i + step) % count))
    return lax.ppermute(value, "tm", pairs)


def strided(value, stride, step):
    total = lax.axis_size("tm")
    rows = total // stride
    pairs = []
    for r in range(rows):
        for j in range(stride):
            pairs.append((r * stride + j, ((r + step) % rows) * stride + j))
    return lax.ppermute(value, "tm", pairs)


def visible(part, label, later):
    total = lax.axis_size("tm")
    row = min(ROW, total)
    rows = total // row
    me = lax.axis_index("tm") // row
    flabel = label.astype(jnp.float32)
    tag = jnp.broadcast_to(flabel, part.shape[:-1] + (1,))
    packed = jnp.concatenate([part, tag], axis=-1)
    frames = [packed] + [shifted(packed, row, s) for s in range(1, row)]
    tags = [f[..., DH + 1 :] for f in frames]
    states = [f[..., : DH + 1] for f in frames]
    keep = [(t >= flabel) if later else (t <= flabel) for t in tags]
    seen = sum(jnp.where(k, s, 0.0) for k, s in zip(keep, states))
    if rows > 1:
        pick = jnp.maximum if later else jnp.minimum
        edge = tags[0]
        for t in tags[1:]:
            edge = pick(edge, t)
        whole = sum(states)
        edge_sum = sum(jnp.where(t == edge, s, 0.0) for t, s in zip(tags, states))
        whole = jnp.concatenate([whole, edge], -1)
        edge_sum = jnp.concatenate([edge_sum, edge], -1)
        for s in range(1, rows):
            target = (me + s) % rows
            sends_whole = (target < me) if later else (target > me)
            got = strided(jnp.where(sends_whole, whole, edge_sum), row, s)
            source = (me - s) % rows
            is_whole = (source > me) if later else (source < me)
            take = is_whole | (got[..., DH + 1 :] == flabel)
            seen = seen + jnp.where(take, got[..., : DH + 1], 0.0)
    return seen.astype(jnp.bfloat16)


def local(query_input, key_input, value_input, cotangent, span_labels):
    groups = lax.axis_size("inner")
    rows, columns = query_input.shape
    width = columns // groups
    heads = width // DH
    tokens = rows * groups

    def to_heads(arrays):
        count = len(arrays)
        outgoing = jnp.stack(arrays).reshape(count, rows, groups, width).transpose(2, 0, 1, 3)
        incoming = lax.all_to_all(outgoing, "inner", 0, 0, tiled=True)
        arrived = incoming.transpose(1, 0, 2, 3).reshape(count, tokens, heads, DH)
        return [arrived[i] for i in range(count)]

    def to_rows(arrays):
        count = len(arrays)
        leaving = jnp.stack(arrays).reshape(count, groups, rows, width).transpose(1, 0, 2, 3)
        returned = lax.all_to_all(leaving, "inner", 0, 0, tiled=True)
        merged = returned.transpose(1, 2, 0, 3).reshape(count, rows, columns)
        return [merged[i] for i in range(count)]

    all_heads = groups * heads
    own_key = key_input.reshape(rows, all_heads, DH)
    own_value = value_input.reshape(rows, all_heads, DH)
    own_feat_key = jnp.maximum(own_key, 0)
    own_ones = jnp.ones((rows, all_heads, 1), jnp.bfloat16)
    own_state = jnp.einsum(
        "thk,thv->hkv",
        own_feat_key,
        jnp.concatenate([own_value, own_ones], axis=-1),
        preferred_element_type=jnp.float32,
    )
    pieces = own_state.astype(jnp.bfloat16).reshape(groups, heads, DH, DH + 1)
    place = lax.axis_index("inner")
    state_part = lax.dynamic_index_in_dim(pieces, place, 0, False).astype(jnp.float32)
    for s in range(1, groups):
        sent = lax.dynamic_index_in_dim(pieces, (place + s) % groups, 0, False)
        got = lax.ppermute(sent, "inner", [(i, (i + s) % groups) for i in range(groups)])
        state_part = state_part + got.astype(jnp.float32)
    feat_query, scaled_heads = to_heads(
        [jnp.maximum(query_input, 0), cotangent * jnp.asarray(loss_scale, jnp.bfloat16)]
    )
    state_part, feat_query, scaled_heads = lax.optimization_barrier(
        (state_part, feat_query, scaled_heads)
    )

    label = span_labels[0]
    state_vis = visible(state_part, label, False)
    both = jnp.einsum("thk,hkv->thv", feat_query, state_vis, preferred_element_type=jnp.float32)
    numerator = both[..., :DH]
    weight = both[..., DH]
    denominator = weight / DH + 1.0
    output = numerator / (DH * denominator[..., None])
    scaled = scaled_heads.astype(jnp.float32)
    numer_back = (scaled / (DH * denominator[..., None])).astype(jnp.bfloat16)
    weight_back = (-jnp.sum(scaled * output, axis=-1) / (DH * denominator)).astype(jnp.bfloat16)
    back_aug = jnp.concatenate([numer_back, weight_back[..., None]], axis=-1)
    adjoint_part = jnp.einsum(
        "thk,thv->hkv", feat_query, back_aug, preferred_element_type=jnp.float32
    )
    query_feat = jnp.einsum("thv,hkv->thk", back_aug, state_vis, preferred_element_type=jnp.float32)
    query_back = jnp.where(feat_query > 0, query_feat, 0.0).astype(jnp.bfloat16)
    adjoint_vis = visible(adjoint_part, label, True)
    (query_out,) = to_rows([query_back])

    copies = jnp.broadcast_to(adjoint_vis[None], (groups,) + adjoint_vis.shape)
    adjoint_all = lax.all_to_all(copies, "inner", 0, 0, tiled=True).reshape(
        groups * heads, DH, DH + 1
    )
    key_feat = jnp.einsum(
        "thv,hkv->thk", own_value, adjoint_all[..., :DH], preferred_element_type=jnp.float32
    ) + adjoint_all[..., DH].astype(jnp.float32)[None]
    value_back = jnp.einsum(
        "thk,hkv->thv", own_feat_key, adjoint_all[..., :DH], preferred_element_type=jnp.float32
    )
    key_out = jnp.where(own_key > 0, key_feat, 0.0).astype(jnp.bfloat16).reshape(rows, columns)
    value_out = value_back.astype(jnp.bfloat16).reshape(rows, columns)
    return query_out, key_out, value_out


def solution(mesh):
    row = P(("tm", "inner"), None)
    return jax.shard_map(
        local,
        mesh=mesh,
        in_specs=(row, row, row, row, P(("tm", "inner"))),
        out_specs=(row, row, row),
        check_vma=False,
    )
```

```python
import jax
import jax.numpy as jnp
from jax import lax
from jax.sharding import PartitionSpec as P

DH = 112

loss_scale = 1024.0


ROW = 8


def shifted(value, count, step):
    total = lax.axis_size("tm")
    pairs = []
    for base in range(0, total, count):
        for i in range(count):
            pairs.append((base + i, base + (i + step) % count))
    return lax.ppermute(value, "tm", pairs)


def strided(value, stride, step):
    total = lax.axis_size("tm")
    rows = total // stride
    pairs = []
    for r in range(rows):
        for j in range(stride):
            pairs.append((r * stride + j, ((r + step) % rows) * stride + j))
    return lax.ppermute(value, "tm", pairs)


def visible(part, label, later):
    total = lax.axis_size("tm")
    row = min(ROW, total)
    rows = total // row
    me = lax.axis_index("tm") // row
    flabel = label.astype(jnp.float32)
    tag = jnp.broadcast_to(flabel, part.shape[:-1] + (1,))
    packed = jnp.concatenate([part, tag], axis=-1)
    frames = [packed] + [shifted(packed, row, s) for s in range(1, row)]
    tags = [f[..., DH + 1 :] for f in frames]
    states = [f[..., : DH + 1] for f in frames]
    keep = [(t >= flabel) if later else (t <= flabel) for t in tags]
    seen = sum(jnp.where(k, s, 0.0) for k, s in zip(keep, states))
    if rows > 1:
        pick = jnp.maximum if later else jnp.minimum
        edge = tags[0]
        for t in tags[1:]:
            edge = pick(edge, t)
        whole = sum(states)
        edge_sum = sum(jnp.where(t == edge, s, 0.0) for t, s in zip(tags, states))
        whole = jnp.concatenate([whole, edge], -1)
        edge_sum = jnp.concatenate([edge_sum, edge], -1)
        for s in range(1, rows):
            target = (me + s) % rows
            sends_whole = (target < me) if later else (target > me)
            got = strided(jnp.where(sends_whole, whole, edge_sum), row, s)
            source = (me - s) % rows
            is_whole = (source > me) if later else (source < me)
            take = is_whole | (got[..., DH + 1 :] == flabel)
            seen = seen + jnp.where(take, got[..., : DH + 1], 0.0)
    return seen.astype(jnp.bfloat16)


def local(query_input, key_input, value_input, cotangent, span_labels):
    groups = lax.axis_size("inner")
    rows, columns = query_input.shape
    width = columns // groups
    heads = width // DH
    tokens = rows * groups

    def to_heads(arrays):
        count = len(arrays)
        outgoing = jnp.stack(arrays).reshape(count, rows, groups, width).transpose(2, 0, 1, 3)
        incoming = lax.all_to_all(outgoing, "inner", 0, 0, tiled=True)
        arrived = incoming.transpose(1, 0, 2, 3).reshape(count, tokens, heads, DH)
        return [arrived[i] for i in range(count)]

    def to_rows(arrays):
        count = len(arrays)
        leaving = jnp.stack(arrays).reshape(count, groups, rows, width).transpose(1, 0, 2, 3)
        returned = lax.all_to_all(leaving, "inner", 0, 0, tiled=True)
        merged = returned.transpose(1, 2, 0, 3).reshape(count, rows, columns)
        return [merged[i] for i in range(count)]

    all_heads = groups * heads
    own_key = key_input.reshape(rows, all_heads, DH)
    own_value = value_input.reshape(rows, all_heads, DH)
    own_feat_key = jnp.maximum(own_key, 0)
    own_ones = jnp.ones((rows, all_heads, 1), jnp.bfloat16)
    own_state = jnp.einsum(
        "thv,thk->vhk",
        jnp.concatenate([own_value, own_ones], axis=-1),
        own_feat_key,
        preferred_element_type=jnp.float32,
    )
    state_rows = own_state.astype(jnp.bfloat16).reshape(DH + 1, groups, width)
    query_rows = jnp.maximum(query_input, 0).reshape(rows, groups, width)
    outgoing = jnp.concatenate([state_rows, query_rows], axis=0).transpose(1, 0, 2)
    incoming = lax.all_to_all(outgoing, "inner", 0, 0, tiled=True)
    summed = jnp.sum(incoming[:, : DH + 1].astype(jnp.float32), axis=0)
    state_part = summed.reshape(DH + 1, heads, DH).transpose(1, 2, 0)
    feat_query = incoming[:, DH + 1 :].reshape(tokens, heads, DH)
    (scaled_heads,) = to_heads([cotangent * jnp.asarray(loss_scale, jnp.bfloat16)])

    label = span_labels[0]
    state_vis = visible(state_part, label, False)
    both = jnp.einsum("thk,hkv->thv", feat_query, state_vis, preferred_element_type=jnp.float32)
    numerator = both[..., :DH]
    weight = both[..., DH]
    denominator = weight / DH + 1.0
    output = numerator / (DH * denominator[..., None])
    scaled = scaled_heads.astype(jnp.float32)
    numer_back = (scaled / (DH * denominator[..., None])).astype(jnp.bfloat16)
    weight_back = (-jnp.sum(scaled * output, axis=-1) / (DH * denominator)).astype(jnp.bfloat16)
    back_aug = jnp.concatenate([numer_back, weight_back[..., None]], axis=-1)
    adjoint_part = jnp.einsum(
        "thk,thv->hkv", feat_query, back_aug, preferred_element_type=jnp.float32
    )
    query_feat = jnp.einsum("thv,hkv->thk", back_aug, state_vis, preferred_element_type=jnp.float32)
    query_back = jnp.where(feat_query > 0, query_feat, 0.0).astype(jnp.bfloat16)
    adjoint_vis = visible(adjoint_part, label, True)
    (query_out,) = to_rows([query_back])

    copies = jnp.broadcast_to(adjoint_vis[None], (groups,) + adjoint_vis.shape)
    adjoint_all = lax.all_to_all(copies, "inner", 0, 0, tiled=True).reshape(
        groups * heads, DH, DH + 1
    )
    key_feat = jnp.einsum(
        "thv,hkv->thk", own_value, adjoint_all[..., :DH], preferred_element_type=jnp.float32
    ) + adjoint_all[..., DH].astype(jnp.float32)[None]
    value_back = jnp.einsum(
        "thk,hkv->thv", own_feat_key, adjoint_all[..., :DH], preferred_element_type=jnp.float32
    )
    key_out = jnp.where(own_key > 0, key_feat, 0.0).astype(jnp.bfloat16).reshape(rows, columns)
    value_out = value_back.astype(jnp.bfloat16).reshape(rows, columns)
    return query_out, key_out, value_out


def solution(mesh):
    row = P(("tm", "inner"), None)
    return jax.shard_map(
        local,
        mesh=mesh,
        in_specs=(row, row, row, row, P(("tm", "inner"))),
        out_specs=(row, row, row),
        check_vma=False,
    )
```

```python
import jax
import jax.numpy as jnp
from jax import lax
from jax.sharding import PartitionSpec as P

DH = 112

loss_scale = 1024.0


ROW = 8


def shifted(value, count, step):
    total = lax.axis_size("tm")
    pairs = []
    for base in range(0, total, count):
        for i in range(count):
            pairs.append((base + i, base + (i + step) % count))
    return lax.ppermute(value, "tm", pairs)


def strided(value, stride, step):
    total = lax.axis_size("tm")
    rows = total // stride
    pairs = []
    for r in range(rows):
        for j in range(stride):
            pairs.append((r * stride + j, ((r + step) % rows) * stride + j))
    return lax.ppermute(value, "tm", pairs)


def visible(part, label, later):
    total = lax.axis_size("tm")
    row = min(ROW, total)
    rows = total // row
    me = lax.axis_index("tm") // row
    flabel = label.astype(jnp.float32)
    tag = jnp.broadcast_to(flabel, part.shape[:-1] + (1,))
    packed = jnp.concatenate([part, tag], axis=-1)
    frames = [packed] + [shifted(packed, row, s) for s in range(1, row)]
    tags = [f[..., DH + 1 :] for f in frames]
    states = [f[..., : DH + 1] for f in frames]
    keep = [(t >= flabel) if later else (t <= flabel) for t in tags]
    seen = sum(jnp.where(k, s, 0.0) for k, s in zip(keep, states))
    if rows > 1:
        pick = jnp.maximum if later else jnp.minimum
        edge = tags[0]
        for t in tags[1:]:
            edge = pick(edge, t)
        whole = sum(states)
        edge_sum = sum(jnp.where(t == edge, s, 0.0) for t, s in zip(tags, states))
        whole = jnp.concatenate([whole, edge], -1)
        edge_sum = jnp.concatenate([edge_sum, edge], -1)
        for s in range(1, rows):
            target = (me + s) % rows
            sends_whole = (target < me) if later else (target > me)
            got = strided(jnp.where(sends_whole, whole, edge_sum), row, s)
            source = (me - s) % rows
            is_whole = (source > me) if later else (source < me)
            take = is_whole | (got[..., DH + 1 :] == flabel)
            seen = seen + jnp.where(take, got[..., : DH + 1], 0.0)
    return seen.astype(jnp.bfloat16)


def local(query_input, key_input, value_input, cotangent, span_labels):
    groups = lax.axis_size("inner")
    rows, columns = query_input.shape
    width = columns // groups
    heads = width // DH
    tokens = rows * groups

    def to_heads(arrays):
        count = len(arrays)
        outgoing = jnp.stack(arrays).reshape(count, rows, groups, width).transpose(2, 0, 1, 3)
        incoming = lax.all_to_all(outgoing, "inner", 0, 0, tiled=True)
        arrived = incoming.transpose(1, 0, 2, 3).reshape(count, tokens, heads, DH)
        return [arrived[i] for i in range(count)]

    def to_rows(arrays):
        count = len(arrays)
        leaving = jnp.stack(arrays).reshape(count, groups, rows, width).transpose(1, 0, 2, 3)
        returned = lax.all_to_all(leaving, "inner", 0, 0, tiled=True)
        merged = returned.transpose(1, 2, 0, 3).reshape(count, rows, columns)
        return [merged[i] for i in range(count)]

    key_heads, value_heads = to_heads([key_input, value_input])
    ones = jnp.ones((tokens, heads, 1), jnp.bfloat16)
    state_part = jnp.einsum(
        "thk,thv->hkv",
        jnp.maximum(key_heads, 0),
        jnp.concatenate([value_heads, ones], axis=-1),
        preferred_element_type=jnp.float32,
    )
    feat_query, scaled_heads = to_heads(
        [jnp.maximum(query_input, 0), cotangent * jnp.asarray(loss_scale, jnp.bfloat16)]
    )

    label = span_labels[0]
    state_vis = visible(state_part, label, False)
    both = jnp.einsum("thk,hkv->thv", feat_query, state_vis, preferred_element_type=jnp.float32)
    numerator = both[..., :DH]
    weight = both[..., DH]
    denominator = weight / DH + 1.0
    output = numerator / (DH * denominator[..., None])
    scaled = scaled_heads.astype(jnp.float32)
    numer_back = (scaled / (DH * denominator[..., None])).astype(jnp.bfloat16)
    weight_back = (-jnp.sum(scaled * output, axis=-1) / (DH * denominator)).astype(jnp.bfloat16)
    back_aug = jnp.concatenate([numer_back, weight_back[..., None]], axis=-1)
    adjoint_part = jnp.einsum(
        "thk,thv->hkv", feat_query, back_aug, preferred_element_type=jnp.float32
    )
    query_feat = jnp.einsum("thv,hkv->thk", back_aug, state_vis, preferred_element_type=jnp.float32)
    query_back = jnp.where(feat_query > 0, query_feat, 0.0).astype(jnp.bfloat16)
    adjoint_vis = visible(adjoint_part, label, True)
    (query_out,) = to_rows([query_back])

    copies = jnp.broadcast_to(adjoint_vis[None], (groups,) + adjoint_vis.shape)
    adjoint_all = lax.all_to_all(copies, "inner", 0, 0, tiled=True).reshape(
        groups * heads, DH, DH + 1
    )
    all_heads = groups * heads
    own_key = key_input.reshape(rows, all_heads, DH)
    own_value = value_input.reshape(rows, all_heads, DH)
    own_feat_key = jnp.maximum(own_key, 0)
    key_feat = jnp.einsum(
        "thv,hkv->thk", own_value, adjoint_all[..., :DH], preferred_element_type=jnp.float32
    ) + adjoint_all[..., DH].astype(jnp.float32)[None]
    value_back = jnp.einsum(
        "thk,hkv->thv", own_feat_key, adjoint_all[..., :DH], preferred_element_type=jnp.float32
    )
    key_out = jnp.where(own_key > 0, key_feat, 0.0).astype(jnp.bfloat16).reshape(rows, columns)
    value_out = value_back.astype(jnp.bfloat16).reshape(rows, columns)
    return query_out, key_out, value_out


def solution(mesh):
    row = P(("tm", "inner"), None)
    return jax.shard_map(
        local,
        mesh=mesh,
        in_specs=(row, row, row, row, P(("tm", "inner"))),
        out_specs=(row, row, row),
        check_vma=False,
    )
```

```python
import jax
import jax.numpy as jnp
from jax import lax
from jax.sharding import PartitionSpec as P

DH = 112

loss_scale = 1024.0


ROW = 4


def shifted(value, count, step):
    total = lax.axis_size("tm")
    pairs = []
    for base in range(0, total, count):
        for i in range(count):
            pairs.append((base + i, base + (i + step) % count))
    return lax.ppermute(value, "tm", pairs)


def strided(value, stride, step):
    total = lax.axis_size("tm")
    rows = total // stride
    pairs = []
    for r in range(rows):
        for j in range(stride):
            pairs.append((r * stride + j, ((r + step) % rows) * stride + j))
    return lax.ppermute(value, "tm", pairs)


def visible(part, label, later):
    total = lax.axis_size("tm")
    row = min(ROW, total)
    rows = total // row
    me = lax.axis_index("tm") // row
    flabel = label.astype(jnp.float32)
    tag = jnp.broadcast_to(flabel, part.shape[:-1] + (1,))
    packed = jnp.concatenate([part, tag], axis=-1)
    frames = [packed] + [shifted(packed, row, s) for s in range(1, row)]
    tags = [f[..., DH + 1 :] for f in frames]
    states = [f[..., : DH + 1] for f in frames]
    keep = [(t >= flabel) if later else (t <= flabel) for t in tags]
    seen = sum(jnp.where(k, s, 0.0) for k, s in zip(keep, states))
    if rows > 1:
        pick = jnp.maximum if later else jnp.minimum
        edge = tags[0]
        for t in tags[1:]:
            edge = pick(edge, t)
        whole = sum(states)
        edge_sum = sum(jnp.where(t == edge, s, 0.0) for t, s in zip(tags, states))
        whole = jnp.concatenate([whole, edge], -1)
        edge_sum = jnp.concatenate([edge_sum, edge], -1)
        for s in range(1, rows):
            target = (me + s) % rows
            sends_whole = (target < me) if later else (target > me)
            got = strided(jnp.where(sends_whole, whole, edge_sum), row, s)
            source = (me - s) % rows
            is_whole = (source > me) if later else (source < me)
            take = is_whole | (got[..., DH + 1 :] == flabel)
            seen = seen + jnp.where(take, got[..., : DH + 1], 0.0)
    return seen.astype(jnp.bfloat16)


def local(query_input, key_input, value_input, cotangent, span_labels):
    groups = lax.axis_size("inner")
    rows, columns = query_input.shape
    width = columns // groups
    heads = width // DH
    tokens = rows * groups

    def to_heads(arrays):
        count = len(arrays)
        outgoing = jnp.stack(arrays).reshape(count, rows, groups, width).transpose(2, 0, 1, 3)
        incoming = lax.all_to_all(outgoing, "inner", 0, 0, tiled=True)
        arrived = incoming.transpose(1, 0, 2, 3).reshape(count, tokens, heads, DH)
        return [arrived[i] for i in range(count)]

    def to_rows(arrays):
        count = len(arrays)
        leaving = jnp.stack(arrays).reshape(count, groups, rows, width).transpose(1, 0, 2, 3)
        returned = lax.all_to_all(leaving, "inner", 0, 0, tiled=True)
        merged = returned.transpose(1, 2, 0, 3).reshape(count, rows, columns)
        return [merged[i] for i in range(count)]

    all_heads = groups * heads
    own_key = key_input.reshape(rows, all_heads, DH)
    own_value = value_input.reshape(rows, all_heads, DH)
    own_feat_key = jnp.maximum(own_key, 0)
    own_ones = jnp.ones((rows, all_heads, 1), jnp.bfloat16)
    own_state = jnp.einsum(
        "thk,thv->hkv",
        own_feat_key,
        jnp.concatenate([own_value, own_ones], axis=-1),
        preferred_element_type=jnp.float32,
    )
    pieces = own_state.astype(jnp.bfloat16).reshape(groups, heads, DH, DH + 1)
    state_part = jnp.sum(
        lax.all_to_all(pieces, "inner", 0, 0, tiled=True).astype(jnp.float32), axis=0
    )
    feat_query, scaled_heads = to_heads(
        [jnp.maximum(query_input, 0), cotangent * jnp.asarray(loss_scale, jnp.bfloat16)]
    )

    label = span_labels[0]
    state_vis = visible(state_part, label, False)
    both = jnp.einsum("thk,hkv->thv", feat_query, state_vis, preferred_element_type=jnp.float32)
    numerator = both[..., :DH]
    weight = both[..., DH]
    denominator = weight / DH + 1.0
    output = numerator / (DH * denominator[..., None])
    scaled = scaled_heads.astype(jnp.float32)
    numer_back = (scaled / (DH * denominator[..., None])).astype(jnp.bfloat16)
    weight_back = (-jnp.sum(scaled * output, axis=-1) / (DH * denominator)).astype(jnp.bfloat16)
    back_aug = jnp.concatenate([numer_back, weight_back[..., None]], axis=-1)
    adjoint_part = jnp.einsum(
        "thk,thv->hkv", feat_query, back_aug, preferred_element_type=jnp.float32
    )
    query_feat = jnp.einsum("thv,hkv->thk", back_aug, state_vis, preferred_element_type=jnp.float32)
    query_back = jnp.where(feat_query > 0, query_feat, 0.0).astype(jnp.bfloat16)
    adjoint_vis = visible(adjoint_part, label, True)
    (query_out,) = to_rows([query_back])

    copies = jnp.broadcast_to(adjoint_vis[None], (groups,) + adjoint_vis.shape)
    adjoint_all = lax.all_to_all(copies, "inner", 0, 0, tiled=True).reshape(
        groups * heads, DH, DH + 1
    )
    key_feat = jnp.einsum(
        "thv,hkv->thk", own_value, adjoint_all[..., :DH], preferred_element_type=jnp.float32
    ) + adjoint_all[..., DH].astype(jnp.float32)[None]
    value_back = jnp.einsum(
        "thk,hkv->thv", own_feat_key, adjoint_all[..., :DH], preferred_element_type=jnp.float32
    )
    key_out = jnp.where(own_key > 0, key_feat, 0.0).astype(jnp.bfloat16).reshape(rows, columns)
    value_out = value_back.astype(jnp.bfloat16).reshape(rows, columns)
    return query_out, key_out, value_out


def solution(mesh):
    row = P(("tm", "inner"), None)
    return jax.shard_map(
        local,
        mesh=mesh,
        in_specs=(row, row, row, row, P(("tm", "inner"))),
        out_specs=(row, row, row),
        check_vma=False,
    )
```

```python
import jax
import jax.numpy as jnp
from jax import lax
from jax.sharding import PartitionSpec as P

DH = 112

loss_scale = 1024.0


ROW = 4


def shifted(value, count, step):
    total = lax.axis_size("tm")
    pairs = []
    for base in range(0, total, count):
        for i in range(count):
            pairs.append((base + i, base + (i + step) % count))
    return lax.ppermute(value, "tm", pairs)


def strided(value, stride, step):
    total = lax.axis_size("tm")
    rows = total // stride
    pairs = []
    for r in range(rows):
        for j in range(stride):
            pairs.append((r * stride + j, ((r + step) % rows) * stride + j))
    return lax.ppermute(value, "tm", pairs)


def visible(part, label, later):
    total = lax.axis_size("tm")
    row = min(ROW, total)
    rows = total // row
    me = lax.axis_index("tm") // row
    flabel = label.astype(jnp.float32)
    tag = jnp.broadcast_to(flabel, part.shape[:-1] + (1,))
    packed = jnp.concatenate([part, tag], axis=-1)
    frames = [packed] + [shifted(packed, row, s) for s in range(1, row)]
    tags = [f[..., DH + 1 :] for f in frames]
    states = [f[..., : DH + 1] for f in frames]
    keep = [(t >= flabel) if later else (t <= flabel) for t in tags]
    seen = sum(jnp.where(k, s, 0.0) for k, s in zip(keep, states))
    if rows > 1:
        pick = jnp.maximum if later else jnp.minimum
        edge = tags[0]
        for t in tags[1:]:
            edge = pick(edge, t)
        whole = sum(states)
        edge_sum = sum(jnp.where(t == edge, s, 0.0) for t, s in zip(tags, states))
        whole = jnp.concatenate([whole, edge], -1)
        edge_sum = jnp.concatenate([edge_sum, edge], -1)
        for s in range(1, rows):
            target = (me + s) % rows
            sends_whole = (target < me) if later else (target > me)
            got = strided(jnp.where(sends_whole, whole, edge_sum), row, s)
            source = (me - s) % rows
            is_whole = (source > me) if later else (source < me)
            take = is_whole | (got[..., DH + 1 :] == flabel)
            seen = seen + jnp.where(take, got[..., : DH + 1], 0.0)
    return seen.astype(jnp.bfloat16)


def local(query_input, key_input, value_input, cotangent, span_labels):
    groups = lax.axis_size("inner")
    rows, columns = query_input.shape
    width = columns // groups
    heads = width // DH
    tokens = rows * groups

    def to_heads(arrays):
        count = len(arrays)
        outgoing = jnp.stack(arrays).reshape(count, rows, groups, width).transpose(2, 0, 1, 3)
        incoming = lax.all_to_all(outgoing, "inner", 0, 0, tiled=True)
        arrived = incoming.transpose(1, 0, 2, 3).reshape(count, tokens, heads, DH)
        return [arrived[i] for i in range(count)]

    def to_rows(arrays):
        count = len(arrays)
        leaving = jnp.stack(arrays).reshape(count, groups, rows, width).transpose(1, 0, 2, 3)
        returned = lax.all_to_all(leaving, "inner", 0, 0, tiled=True)
        merged = returned.transpose(1, 2, 0, 3).reshape(count, rows, columns)
        return [merged[i] for i in range(count)]

    key_heads, value_heads = to_heads([key_input, value_input])
    ones = jnp.ones((tokens, heads, 1), jnp.bfloat16)
    state_part = jnp.einsum(
        "thk,thv->hkv",
        jnp.maximum(key_heads, 0),
        jnp.concatenate([value_heads, ones], axis=-1),
        preferred_element_type=jnp.float32,
    )
    feat_query, scaled_heads = to_heads(
        [jnp.maximum(query_input, 0), cotangent * jnp.asarray(loss_scale, jnp.bfloat16)]
    )

    label = span_labels[0]
    state_vis = visible(state_part, label, False)
    both = jnp.einsum("thk,hkv->thv", feat_query, state_vis, preferred_element_type=jnp.float32)
    numerator = both[..., :DH]
    weight = both[..., DH]
    denominator = weight / DH + 1.0
    output = numerator / (DH * denominator[..., None])
    scaled = scaled_heads.astype(jnp.float32)
    numer_back = (scaled / (DH * denominator[..., None])).astype(jnp.bfloat16)
    weight_back = (-jnp.sum(scaled * output, axis=-1) / (DH * denominator)).astype(jnp.bfloat16)
    back_aug = jnp.concatenate([numer_back, weight_back[..., None]], axis=-1)
    adjoint_part = jnp.einsum(
        "thk,thv->hkv", feat_query, back_aug, preferred_element_type=jnp.float32
    )
    query_feat = jnp.einsum("thv,hkv->thk", back_aug, state_vis, preferred_element_type=jnp.float32)
    query_back = jnp.where(feat_query > 0, query_feat, 0.0).astype(jnp.bfloat16)
    adjoint_vis = visible(adjoint_part, label, True)
    (query_out,) = to_rows([query_back])

    copies = jnp.broadcast_to(adjoint_vis[None], (groups,) + adjoint_vis.shape)
    adjoint_all = lax.all_to_all(copies, "inner", 0, 0, tiled=True).reshape(
        groups * heads, DH, DH + 1
    )
    all_heads = groups * heads
    own_key = key_input.reshape(rows, all_heads, DH)
    own_value = value_input.reshape(rows, all_heads, DH)
    own_feat_key = jnp.maximum(own_key, 0)
    key_feat = jnp.einsum(
        "thv,hkv->thk", own_value, adjoint_all[..., :DH], preferred_element_type=jnp.float32
    ) + adjoint_all[..., DH].astype(jnp.float32)[None]
    value_back = jnp.einsum(
        "thk,hkv->thv", own_feat_key, adjoint_all[..., :DH], preferred_element_type=jnp.float32
    )
    key_out = jnp.where(own_key > 0, key_feat, 0.0).astype(jnp.bfloat16).reshape(rows, columns)
    value_out = value_back.astype(jnp.bfloat16).reshape(rows, columns)
    return query_out, key_out, value_out


def solution(mesh):
    row = P(("tm", "inner"), None)
    return jax.shard_map(
        local,
        mesh=mesh,
        in_specs=(row, row, row, row, P(("tm", "inner"))),
        out_specs=(row, row, row),
        check_vma=False,
    )
```

```python
import jax
import jax.numpy as jnp
from jax import lax
from jax.sharding import PartitionSpec as P

DH = 112

loss_scale = 1024.0


ROW = 2


def shifted(value, count, step):
    total = lax.axis_size("tm")
    pairs = []
    for base in range(0, total, count):
        for i in range(count):
            pairs.append((base + i, base + (i + step) % count))
    return lax.ppermute(value, "tm", pairs)


def strided(value, stride, step):
    total = lax.axis_size("tm")
    rows = total // stride
    pairs = []
    for r in range(rows):
        for j in range(stride):
            pairs.append((r * stride + j, ((r + step) % rows) * stride + j))
    return lax.ppermute(value, "tm", pairs)


def visible(part, label, later):
    total = lax.axis_size("tm")
    row = min(ROW, total)
    rows = total // row
    me = lax.axis_index("tm") // row
    flabel = label.astype(jnp.float32)
    tag = jnp.broadcast_to(flabel, part.shape[:-1] + (1,))
    packed = jnp.concatenate([part, tag], axis=-1)
    frames = [packed] + [shifted(packed, row, s) for s in range(1, row)]
    tags = [f[..., DH + 1 :] for f in frames]
    states = [f[..., : DH + 1] for f in frames]
    keep = [(t >= flabel) if later else (t <= flabel) for t in tags]
    seen = sum(jnp.where(k, s, 0.0) for k, s in zip(keep, states))
    if rows > 1:
        pick = jnp.maximum if later else jnp.minimum
        edge = tags[0]
        for t in tags[1:]:
            edge = pick(edge, t)
        whole = sum(states)
        edge_sum = sum(jnp.where(t == edge, s, 0.0) for t, s in zip(tags, states))
        whole = jnp.concatenate([whole, edge], -1)
        edge_sum = jnp.concatenate([edge_sum, edge], -1)
        for s in range(1, rows):
            target = (me + s) % rows
            sends_whole = (target < me) if later else (target > me)
            got = strided(jnp.where(sends_whole, whole, edge_sum), row, s)
            source = (me - s) % rows
            is_whole = (source > me) if later else (source < me)
            take = is_whole | (got[..., DH + 1 :] == flabel)
            seen = seen + jnp.where(take, got[..., : DH + 1], 0.0)
    return seen.astype(jnp.bfloat16)


def local(query_input, key_input, value_input, cotangent, span_labels):
    groups = lax.axis_size("inner")
    rows, columns = query_input.shape
    width = columns // groups
    heads = width // DH
    tokens = rows * groups

    def to_heads(arrays):
        count = len(arrays)
        outgoing = jnp.stack(arrays).reshape(count, rows, groups, width).transpose(2, 0, 1, 3)
        incoming = lax.all_to_all(outgoing, "inner", 0, 0, tiled=True)
        arrived = incoming.transpose(1, 0, 2, 3).reshape(count, tokens, heads, DH)
        return [arrived[i] for i in range(count)]

    def to_rows(arrays):
        count = len(arrays)
        leaving = jnp.stack(arrays).reshape(count, groups, rows, width).transpose(1, 0, 2, 3)
        returned = lax.all_to_all(leaving, "inner", 0, 0, tiled=True)
        merged = returned.transpose(1, 2, 0, 3).reshape(count, rows, columns)
        return [merged[i] for i in range(count)]

    all_heads = groups * heads
    own_key = key_input.reshape(rows, all_heads, DH)
    own_value = value_input.reshape(rows, all_heads, DH)
    own_feat_key = jnp.maximum(own_key, 0)
    own_ones = jnp.ones((rows, all_heads, 1), jnp.bfloat16)
    own_state = jnp.einsum(
        "thk,thv->hkv",
        own_feat_key,
        jnp.concatenate([own_value, own_ones], axis=-1),
        preferred_element_type=jnp.float32,
    )
    pieces = own_state.astype(jnp.bfloat16).reshape(groups, heads, DH, DH + 1)
    state_part = jnp.sum(
        lax.all_to_all(pieces, "inner", 0, 0, tiled=True).astype(jnp.float32), axis=0
    )
    feat_query, scaled_heads = to_heads(
        [jnp.maximum(query_input, 0), cotangent * jnp.asarray(loss_scale, jnp.bfloat16)]
    )

    label = span_labels[0]
    state_vis = visible(state_part, label, False)
    both = jnp.einsum("thk,hkv->thv", feat_query, state_vis, preferred_element_type=jnp.float32)
    numerator = both[..., :DH]
    weight = both[..., DH]
    denominator = weight / DH + 1.0
    output = numerator / (DH * denominator[..., None])
    scaled = scaled_heads.astype(jnp.float32)
    numer_back = (scaled / (DH * denominator[..., None])).astype(jnp.bfloat16)
    weight_back = (-jnp.sum(scaled * output, axis=-1) / (DH * denominator)).astype(jnp.bfloat16)
    back_aug = jnp.concatenate([numer_back, weight_back[..., None]], axis=-1)
    adjoint_part = jnp.einsum(
        "thk,thv->hkv", feat_query, back_aug, preferred_element_type=jnp.float32
    )
    query_feat = jnp.einsum("thv,hkv->thk", back_aug, state_vis, preferred_element_type=jnp.float32)
    query_back = jnp.where(feat_query > 0, query_feat, 0.0).astype(jnp.bfloat16)
    adjoint_vis = visible(adjoint_part, label, True)
    (query_out,) = to_rows([query_back])

    copies = jnp.broadcast_to(adjoint_vis[None], (groups,) + adjoint_vis.shape)
    adjoint_all = lax.all_to_all(copies, "inner", 0, 0, tiled=True).reshape(
        groups * heads, DH, DH + 1
    )
    key_feat = jnp.einsum(
        "thv,hkv->thk", own_value, adjoint_all[..., :DH], preferred_element_type=jnp.float32
    ) + adjoint_all[..., DH].astype(jnp.float32)[None]
    value_back = jnp.einsum(
        "thk,hkv->thv", own_feat_key, adjoint_all[..., :DH], preferred_element_type=jnp.float32
    )
    key_out = jnp.where(own_key > 0, key_feat, 0.0).astype(jnp.bfloat16).reshape(rows, columns)
    value_out = value_back.astype(jnp.bfloat16).reshape(rows, columns)
    return query_out, key_out, value_out


def solution(mesh):
    row = P(("tm", "inner"), None)
    return jax.shard_map(
        local,
        mesh=mesh,
        in_specs=(row, row, row, row, P(("tm", "inner"))),
        out_specs=(row, row, row),
        check_vma=False,
    )
```

```python
import jax
import jax.numpy as jnp
from jax import lax
from jax.sharding import PartitionSpec as P

DH = 112

loss_scale = 1024.0


ROW = 4


def shifted(value, count, step):
    total = lax.axis_size("tm")
    pairs = []
    for base in range(0, total, count):
        for i in range(count):
            pairs.append((base + i, base + (i + step) % count))
    return lax.ppermute(value, "tm", pairs)


def strided(value, stride, step):
    total = lax.axis_size("tm")
    rows = total // stride
    pairs = []
    for r in range(rows):
        for j in range(stride):
            pairs.append((r * stride + j, ((r + step) % rows) * stride + j))
    return lax.ppermute(value, "tm", pairs)


def visible(part, label, later):
    total = lax.axis_size("tm")
    row = min(ROW, total)
    rows = total // row
    me = lax.axis_index("tm") // row
    flabel = label.astype(jnp.float32)
    tag = jnp.broadcast_to(flabel, part.shape[:-1] + (1,))
    packed = jnp.concatenate([part, tag], axis=-1)
    frames = [packed] + [shifted(packed, row, s) for s in range(1, row)]
    tags = [f[..., DH + 1 :] for f in frames]
    states = [f[..., : DH + 1] for f in frames]
    keep = [(t >= flabel) if later else (t <= flabel) for t in tags]
    seen = sum(jnp.where(k, s, 0.0) for k, s in zip(keep, states))
    if rows > 1:
        pick = jnp.maximum if later else jnp.minimum
        edge = tags[0]
        for t in tags[1:]:
            edge = pick(edge, t)
        whole = sum(states)
        edge_sum = sum(jnp.where(t == edge, s, 0.0) for t, s in zip(tags, states))
        whole = jnp.concatenate([whole, edge], -1)
        edge_sum = jnp.concatenate([edge_sum, edge], -1)
        for s in range(1, rows):
            target = (me + s) % rows
            sends_whole = (target < me) if later else (target > me)
            got = strided(jnp.where(sends_whole, whole, edge_sum), row, s)
            source = (me - s) % rows
            is_whole = (source > me) if later else (source < me)
            take = is_whole | (got[..., DH + 1 :] == flabel)
            seen = seen + jnp.where(take, got[..., : DH + 1], 0.0)
    return seen.astype(jnp.bfloat16)


def local(query_input, key_input, value_input, cotangent, span_labels):
    groups = lax.axis_size("inner")
    rows, columns = query_input.shape
    width = columns // groups
    heads = width // DH
    tokens = rows * groups

    def to_heads(arrays):
        count = len(arrays)
        outgoing = jnp.stack(arrays).reshape(count, rows, groups, width).transpose(2, 0, 1, 3)
        incoming = lax.all_to_all(outgoing, "inner", 0, 0, tiled=True)
        arrived = incoming.transpose(1, 0, 2, 3).reshape(count, tokens, heads, DH)
        return [arrived[i] for i in range(count)]

    def to_rows(arrays):
        count = len(arrays)
        leaving = jnp.stack(arrays).reshape(count, groups, rows, width).transpose(1, 0, 2, 3)
        returned = lax.all_to_all(leaving, "inner", 0, 0, tiled=True)
        merged = returned.transpose(1, 2, 0, 3).reshape(count, rows, columns)
        return [merged[i] for i in range(count)]

    all_heads = groups * heads
    own_key = key_input.reshape(rows, all_heads, DH)
    own_value = value_input.reshape(rows, all_heads, DH)
    own_feat_key = jnp.maximum(own_key, 0)
    own_state = jnp.concatenate(
        [
            jnp.einsum("thk,thv->hkv", own_feat_key, own_value, preferred_element_type=jnp.float32),
            jnp.sum(own_feat_key, axis=0, dtype=jnp.float32)[..., None],
        ],
        axis=-1,
    )
    pieces = own_state.astype(jnp.bfloat16).reshape(groups, heads, DH, DH + 1)
    state_part = jnp.sum(
        lax.all_to_all(pieces, "inner", 0, 0, tiled=True).astype(jnp.float32), axis=0
    )
    feat_query, scaled_heads = to_heads(
        [jnp.maximum(query_input, 0), cotangent * jnp.asarray(loss_scale, jnp.bfloat16)]
    )

    label = span_labels[0]
    state_vis = visible(state_part, label, False)
    both = jnp.einsum("thk,hkv->thv", feat_query, state_vis, preferred_element_type=jnp.float32)
    numerator = both[..., :DH]
    weight = both[..., DH]
    denominator = weight / DH + 1.0
    output = numerator / (DH * denominator[..., None])
    scaled = scaled_heads.astype(jnp.float32)
    numer_back = (scaled / (DH * denominator[..., None])).astype(jnp.bfloat16)
    weight_back = (-jnp.sum(scaled * output, axis=-1) / (DH * denominator)).astype(jnp.bfloat16)
    back_aug = jnp.concatenate([numer_back, weight_back[..., None]], axis=-1)
    adjoint_part = jnp.einsum(
        "thk,thv->hkv", feat_query, back_aug, preferred_element_type=jnp.float32
    )
    query_feat = jnp.einsum("thv,hkv->thk", back_aug, state_vis, preferred_element_type=jnp.float32)
    query_back = jnp.where(feat_query > 0, query_feat, 0.0).astype(jnp.bfloat16)
    adjoint_vis = visible(adjoint_part, label, True)
    (query_out,) = to_rows([query_back])

    copies = jnp.broadcast_to(adjoint_vis[None], (groups,) + adjoint_vis.shape)
    adjoint_all = lax.all_to_all(copies, "inner", 0, 0, tiled=True).reshape(
        groups * heads, DH, DH + 1
    )
    key_feat = jnp.einsum(
        "thv,hkv->thk", own_value, adjoint_all[..., :DH], preferred_element_type=jnp.float32
    ) + adjoint_all[..., DH].astype(jnp.float32)[None]
    value_back = jnp.einsum(
        "thk,hkv->thv", own_feat_key, adjoint_all[..., :DH], preferred_element_type=jnp.float32
    )
    key_out = jnp.where(own_key > 0, key_feat, 0.0).astype(jnp.bfloat16).reshape(rows, columns)
    value_out = value_back.astype(jnp.bfloat16).reshape(rows, columns)
    return query_out, key_out, value_out


def solution(mesh):
    row = P(("tm", "inner"), None)
    return jax.shard_map(
        local,
        mesh=mesh,
        in_specs=(row, row, row, row, P(("tm", "inner"))),
        out_specs=(row, row, row),
        check_vma=False,
    )
```
